32 devices in a mesh: sector: 8 (over y, x, core), sub: 4 (over z).
Axes of the slice: x: 2, y: 2, z: 4, core: 2. Of those that a mesh axis runs over, the one named last changes fastest.
Arguments:
- dual_load: float32 [8, 4, 2, 512, 256], P('sector', 'sub'), may hold values from -50 to 50
- flexibility: bfloat16 [8, 4, 2048, 2048], P('sector', 'sub'), may hold values from -10 to 10, as said below
- face_order: int32 [8, 4, 2048], P('sector', 'sub'), may hold values from 0 to 2047, each once within a row
- corner_index: int32 [8, 4, 32], P('sector', 'sub'), may hold values from 0 to 2047, as said below
- coarse_inverse: float32 [256, 256], replicated, may hold values from -10 to 10, as said below
Outputs:
- multiplier: float32 [8, 4, 2, 512, 256], P('sector', 'sub')
- residual: float32 [8, 4, 2, 512, 256], P('sector', 'sub')
The draws below stay inside these ranges and needn't reach their ends.
Inputs may be any that keep to these rules, and one draw needn't show every extreme that they name: `flexibility`: a block of sizes of order one with a dominant diagonal; each subdomain's matrix is symmetric positive definite. `corner_index`: entries within one subdomain are distinct. `face_order`: each subdomain's row names every face slot once. `coarse_inverse`: symmetric positive definite with a dominant diagonal.
All inputs are finite; a program needn't handle non-finite values.
Results may differ from the reference program's by a relative error of at most 0.0087.
The reference program's roundings to bfloat16 on the way count: a program that leaves them out, or rounds other values in their place, can miss the bound.
Values may be sent and summed in bfloat16 or wider, within the bound.
No kernel may reach another device: no remote copies, remote signals or barrier semaphores. Data moves between devices by JAX's collectives and lax.ppermute only.
A program may use at most 128 MiB of HBM per device.

```python
import math
import jax
import jax.numpy as jnp
from jax import lax

NI = 2048
NC = 32
R = 256
ITERS = 2
M = 512
SECTORS = 8
SUBS = 4


def draw_dual_load(key, part):
    first, second = jax.random.split(key, 2)
    shape = (SECTORS, SUBS, 2, M, R)
    position = (jnp.arange(SECTORS)[:, None] * SUBS + jnp.arange(SUBS)[None, :]).astype(jnp.float32)
    factor = 1.0 + 2.0 * position / max(SECTORS * SUBS - 1, 1)
    column = jnp.exp(jax.random.uniform(second, (R,), minval=math.log(0.3), maxval=math.log(3.0)))
    base = jax.random.normal(first, shape)
    values = base * factor[:, :, None, None, None] * column
    return jnp.clip(values, -50.0, 50.0).astype(jnp.float32)


def draw_flexibility(key, part):
    first, second, third = jax.random.split(key, 3)
    shape = (SECTORS, SUBS, NI, NI)
    spread = 0.3 / math.sqrt(NI)
    noise = jax.random.normal(first, shape) * spread
    scales = jnp.exp(jax.random.uniform(second, (SECTORS, SUBS, NI), minval=math.log(0.7), maxval=math.log(1.4)))
    symmetric = (noise + jnp.swapaxes(noise, 2, 3)) / math.sqrt(2.0)
    diagonal = jax.random.uniform(third, (SECTORS, SUBS, NI), minval=1.0, maxval=2.0)
    identity = (jnp.arange(NI)[:, None] == jnp.arange(NI)[None, :]).astype(jnp.float32)
    matrix = symmetric + identity * diagonal[:, :, :, None]
    matrix = matrix * scales[:, :, :, None] * scales[:, :, None, :]
    return jnp.clip(matrix, -10.0, 10.0).astype(jnp.bfloat16)


def draw_corner_index(key, part):
    scores = jax.random.randint(key, (SECTORS, SUBS, NI), 0, 2 ** 19)
    scores = scores * NI + jnp.arange(NI, dtype=jnp.int32)
    ranked = jnp.argsort(scores, axis=-1, stable=True)
    return ranked[:, :, :NC].astype(jnp.int32)


def draw_coarse_inverse(key, part):
    first, second = jax.random.split(jax.random.fold_in(key, 7))
    total = SECTORS * NC
    spread = 0.3 / math.sqrt(total)
    noise = jax.random.normal(first, (total, total)) * spread
    symmetric = (noise + noise.T) / math.sqrt(2.0)
    diagonal = jax.random.uniform(second, (total,), minval=1.0, maxval=2.0)
    identity = (jnp.arange(total)[:, None] == jnp.arange(total)[None, :]).astype(jnp.float32)
    matrix = symmetric + identity * diagonal[:, None]
    return jnp.clip(matrix, -10.0, 10.0).astype(jnp.float32)


def setup_inputs(seed: int = 0) -> dict:
    seeds = jax.random.split(jax.random.key(seed), 6)
    dual_load = draw_dual_load(jax.random.fold_in(seeds[5], 71), 0)
    flexibility = draw_flexibility(jax.random.fold_in(seeds[5], 71), 0)
    face_order = jax.vmap(lambda own: jax.random.permutation(own, NI))(jax.random.split(seeds[2], SECTORS * SUBS)).reshape((SECTORS, SUBS, NI)).astype(jnp.int32)
    corner_index = draw_corner_index(jax.random.fold_in(seeds[5], 71), 0)
    coarse_inverse = draw_coarse_inverse(jax.random.fold_in(seeds[5], 71), 0)
    return {"dual_load": dual_load, "flexibility": flexibility, "face_order": face_order, "corner_index": corner_index, "coarse_inverse": coarse_inverse}


def local_product(operands):
    matrix, slot_order, face_stack = operands
    reordered = jnp.take(jnp.take(matrix, slot_order, axis=0), slot_order, axis=1)
    return jnp.dot(reordered.astype(jnp.float32), face_stack.astype(jnp.float32), precision=lax.Precision.HIGHEST, preferred_element_type=jnp.float32)


def add_corner(target, corner_slots, coarse_add):
    return target.at[corner_slots].add(coarse_add)


def apply_operator(direction, flexibility, face_order, corner_index, coarse_inverse):
    rounded = direction.astype(jnp.bfloat16)
    lam_sub = rounded[:, :, 0]
    lam_cycle = rounded[:, :, 1]
    lower_sub = jnp.concatenate([jnp.zeros_like(lam_sub[:, :1]), lam_sub[:, :-1]], axis=1)
    previous = jnp.roll(lam_cycle, 1, axis=0)
    face_stack = jnp.concatenate([-lower_sub, lam_sub, -previous, lam_cycle], axis=2)
    flat_faces = face_stack.reshape(SECTORS * SUBS, 4 * M, R)
    flat_matrix = flexibility.reshape(SECTORS * SUBS, 4 * M, 4 * M)
    flat_order = face_order.reshape(SECTORS * SUBS, 4 * M)
    product = lax.map(local_product, (flat_matrix, flat_order, flat_faces))
    flat_corner = corner_index.reshape(SECTORS * SUBS, -1)
    partial_value = jnp.take_along_axis(flat_faces, flat_corner[:, :, None], axis=1).astype(jnp.float32)
    sector_corner = jnp.sum(partial_value.reshape(SECTORS, SUBS, NC, R), axis=1)
    stacked = sector_corner.reshape(SECTORS * NC, R)
    coarse = jnp.dot(coarse_inverse, stacked, precision=lax.Precision.HIGHEST, preferred_element_type=jnp.float32) / SUBS
    coarse_add = jnp.repeat(coarse.reshape(SECTORS, NC, R), SUBS, axis=0)
    image_rows = jax.vmap(add_corner)(product, flat_corner, coarse_add).reshape(SECTORS, SUBS, 4, M, R)
    sent = lax.optimization_barrier(image_rows.astype(jnp.bfloat16)).astype(jnp.float32)
    next_lower = jnp.concatenate([sent[:, 1:, 0], jnp.zeros_like(sent[:, :1, 0])], axis=1)
    jump_sub = image_rows[:, :, 1] - next_lower
    jump_cycle = image_rows[:, :, 3] - jnp.roll(sent[:, :, 2], -1, axis=0)
    return jnp.stack([jump_sub, jump_cycle], axis=2)


def reference(dual_load, flexibility, face_order, corner_index, coarse_inverse):
    multiplier = jnp.zeros_like(dual_load)
    residual = dual_load
    direction = dual_load
    norm_now = jnp.sum(residual * residual, axis=(0, 1, 2, 3))
    for iteration in range(ITERS):
        image = apply_operator(direction, flexibility, face_order, corner_index, coarse_inverse)
        alpha = norm_now / jnp.sum(direction * image, axis=(0, 1, 2, 3))
        multiplier = multiplier + alpha * direction
        residual = residual - alpha * image
        if iteration + 1 < ITERS:
            norm_next = jnp.sum(residual * residual, axis=(0, 1, 2, 3))
            direction = residual + (norm_next / norm_now) * direction
            norm_now = norm_next
    return multiplier, residual
```

```python
import jax
import jax.numpy as jnp
from jax import lax
from jax.sharding import PartitionSpec as P

ITERS = 2


def passed_along(x, axis, by):
    count = lax.axis_size(axis)
    pairs = [(i, i + by) for i in range(count) if 0 <= i + by < count]
    return lax.ppermute(x, axis, pairs)


def from_behind(value, axis, steps):
    count = lax.axis_size(axis)
    pairs = [(source, (source + steps) % count) for source in range(count)]
    return lax.ppermute(value, axis, pairs)


def squares(residual):
    return lax.psum(jnp.sum(residual * residual, axis=(0, 1, 2, 3)), ("sector", "sub"))


def inner_sum(left, right):
    return jnp.sum(left * right, axis=(0, 1, 2, 3))


def shards(dual_load, flexibility, face_order, corner_index, coarse_inverse):
    slot_order = face_order[0, 0]
    corners = corner_index[0, 0]
    corner_count = corners.shape[0]
    slot_count = slot_order.shape[0]
    own_place = jnp.zeros((slot_count,), jnp.int32).at[slot_order].set(jnp.arange(slot_count, dtype=jnp.int32))
    matrix = flexibility[0, 0]
    face_width = slot_order.shape[0] // 4
    cases = dual_load.shape[-1]
    sub_count = lax.axis_size("sub")
    multiplier = jnp.zeros_like(dual_load)
    residual = dual_load
    direction = dual_load
    norm_now = squares(residual)
    for iteration in range(ITERS):
        rounded = direction[0, 0].astype(jnp.bfloat16)
        lower_sub = passed_along(rounded[0], "sub", 1)
        previous = from_behind(rounded[1], "sector", 1)
        face_stack = jnp.concatenate([-lower_sub, rounded[0], -previous, rounded[1]], axis=0)
        partial_value = jnp.take(face_stack, corners, axis=0).astype(jnp.float32)
        sector_total = lax.psum(partial_value.astype(jnp.bfloat16), "sub").astype(jnp.float32)
        sector_id = lax.axis_index("sector")
        everything = lax.all_gather(sector_total, "sector", axis=0, tiled=True)
        inverse_rows = lax.dynamic_slice_in_dim(
            coarse_inverse, sector_id * corner_count, corner_count, 0
        )
        coarse = jnp.dot(
            inverse_rows,
            everything,
            precision=lax.Precision.HIGHEST,
            preferred_element_type=jnp.float32,
        )
        coarse = coarse / sub_count
        correction = jnp.zeros((4 * face_width, cases), jnp.float32).at[corners].add(coarse)
        own_faces = jnp.take(face_stack, own_place, axis=0)
        own_product = jnp.dot(matrix, own_faces, preferred_element_type=jnp.float32)
        product = jnp.take(own_product, slot_order, axis=0) + correction
        outgoing_sub = product[:face_width]
        outgoing_cycle = product[2 * face_width : 3 * face_width]
        upper_next = passed_along(outgoing_sub.astype(jnp.bfloat16), "sub", -1)
        cycle_next = from_behind(outgoing_cycle.astype(jnp.bfloat16), "sector", -1)
        own_sub = product[face_width : 2 * face_width]
        own_cycle = product[3 * face_width :]
        jump_pair = jnp.stack(
            [own_sub - upper_next.astype(jnp.float32), own_cycle - cycle_next.astype(jnp.float32)],
            axis=0,
        )
        image = jump_pair[None, None]
        curvature = lax.psum(inner_sum(direction, image), ("sector", "sub"))
        alpha = norm_now / curvature
        multiplier = multiplier + alpha * direction
        residual = residual - alpha * image
        if iteration + 1 < ITERS:
            norm_next = squares(residual)
            direction = residual + norm_next / norm_now * direction
            norm_now = norm_next
    return (multiplier, residual)


def solution(mesh):
    return jax.shard_map(
        shards,
        mesh=mesh,
        in_specs=(
            P("sector", "sub", None, None, None),
            P("sector", "sub", None, None),
            P("sector", "sub", None),
            P("sector", "sub", None),
            P(),
        ),
        out_specs=(P("sector", "sub", None, None, None), P("sector", "sub", None, None, None)),
        check_vma=False,
    )
```

```python
import jax
import jax.numpy as jnp
from jax import lax
from jax.sharding import PartitionSpec as P

ITERS = 2


def passed_along(x, axis, by):
    count = lax.axis_size(axis)
    pairs = [(i, i + by) for i in range(count) if 0 <= i + by < count]
    return lax.ppermute(x, axis, pairs)


def from_behind(value, axis, steps):
    count = lax.axis_size(axis)
    pairs = [(source, (source + steps) % count) for source in range(count)]
    return lax.ppermute(value, axis, pairs)


def total(x):
    for axis in ("sub", "sector"):
        count = lax.axis_size(axis)
        if count & (count - 1):
            x = lax.psum(x, axis)
            continue
        step = 1
        while step < count:
            x = x + lax.ppermute(x, axis, [(i, i ^ step) for i in range(count)])
            step *= 2
    return x


def squares(residual):
    return total(jnp.sum(residual * residual, axis=(0, 1, 2, 3)))


def inner_sum(left, right):
    return jnp.sum(left * right, axis=(0, 1, 2, 3))


def shards(dual_load, flexibility, face_order, corner_index, coarse_inverse):
    slot_order = face_order[0, 0]
    corners = corner_index[0, 0]
    corner_count = corners.shape[0]
    slot_count = slot_order.shape[0]
    own_place = jnp.zeros((slot_count,), jnp.int32).at[slot_order].set(jnp.arange(slot_count, dtype=jnp.int32))
    matrix = flexibility[0, 0]
    face_width = slot_order.shape[0] // 4
    cases = dual_load.shape[-1]
    sub_count = lax.axis_size("sub")
    multiplier = jnp.zeros_like(dual_load)
    residual = dual_load
    direction = dual_load
    for iteration in range(ITERS):
        rounded = direction[0, 0].astype(jnp.bfloat16)
        lower_sub = passed_along(rounded[0], "sub", 1)
        previous = from_behind(rounded[1], "sector", 1)
        face_stack = jnp.concatenate([-lower_sub, rounded[0], -previous, rounded[1]], axis=0)
        partial_value = jnp.take(face_stack, corners, axis=0).astype(jnp.float32)
        sector_total = lax.psum(partial_value.astype(jnp.bfloat16), "sub").astype(jnp.float32)
        sector_id = lax.axis_index("sector")
        everything = lax.all_gather(sector_total, "sector", axis=0, tiled=True)
        inverse_rows = lax.dynamic_slice_in_dim(
            coarse_inverse, sector_id * corner_count, corner_count, 0
        )
        coarse = jnp.dot(
            inverse_rows,
            everything,
            precision=lax.Precision.HIGHEST,
            preferred_element_type=jnp.float32,
        )
        coarse = coarse / sub_count
        correction = jnp.zeros((4 * face_width, cases), jnp.float32).at[corners].add(coarse)
        own_faces = jnp.take(face_stack, own_place, axis=0)
        own_product = jnp.dot(matrix, own_faces, preferred_element_type=jnp.float32)
        product = jnp.take(own_product, slot_order, axis=0) + correction
        outgoing_sub = product[:face_width]
        outgoing_cycle = product[2 * face_width : 3 * face_width]
        upper_next = passed_along(outgoing_sub.astype(jnp.bfloat16), "sub", -1)
        cycle_next = from_behind(outgoing_cycle.astype(jnp.bfloat16), "sector", -1)
        own_sub = product[face_width : 2 * face_width]
        own_cycle = product[3 * face_width :]
        jump_pair = jnp.stack(
            [own_sub - upper_next.astype(jnp.float32), own_cycle - cycle_next.astype(jnp.float32)],
            axis=0,
        )
        image = jump_pair[None, None]
        if iteration == 0:
            both = total(jnp.stack([inner_sum(residual, residual), inner_sum(direction, image)]))
            norm_now, curvature = both[0], both[1]
        else:
            curvature = total(inner_sum(direction, image))
        alpha = norm_now / curvature
        multiplier = multiplier + alpha * direction
        residual = residual - alpha * image
        if iteration + 1 < ITERS:
            norm_next = squares(residual)
            direction = residual + norm_next / norm_now * direction
            norm_now = norm_next
    return (multiplier, residual)


def solution(mesh):
    return jax.shard_map(
        shards,
        mesh=mesh,
        in_specs=(
            P("sector", "sub", None, None, None),
            P("sector", "sub", None, None),
            P("sector", "sub", None),
            P("sector", "sub", None),
            P(),
        ),
        out_specs=(P("sector", "sub", None, None, None), P("sector", "sub", None, None, None)),
        check_vma=False,
    )
```

```python
import jax
import jax.numpy as jnp
from jax import lax
from jax.sharding import PartitionSpec as P

ITERS = 2


def passed_along(x, axis, by):
    count = lax.axis_size(axis)
    pairs = [(i, i + by) for i in range(count) if 0 <= i + by < count]
    return lax.ppermute(x, axis, pairs)


def from_behind(value, axis, steps):
    count = lax.axis_size(axis)
    pairs = [(source, (source + steps) % count) for source in range(count)]
    return lax.ppermute(value, axis, pairs)


def total(x):
    for axis in ("sub", "sector"):
        count = lax.axis_size(axis)
        if count & (count - 1):
            x = lax.psum(x, axis)
            continue
        step = 1
        while step < count:
            x = x + lax.ppermute(x, axis, [(i, i ^ step) for i in range(count)])
            step *= 2
    return x


def gathered(x, axis):
    count = lax.axis_size(axis)
    return [x] + [
        lax.ppermute(x, axis, [(i, (i + k) % count) for i in range(count)]) for k in range(1, count)
    ]


def squares(residual):
    return total(jnp.sum(residual * residual, axis=(0, 1, 2, 3)))


def inner_sum(left, right):
    return jnp.sum(left * right, axis=(0, 1, 2, 3))


def shards(dual_load, flexibility, face_order, corner_index, coarse_inverse):
    slot_order = face_order[0, 0]
    corners = corner_index[0, 0]
    corner_count = corners.shape[0]
    slot_count = slot_order.shape[0]
    own_place = jnp.zeros((slot_count,), jnp.int32).at[slot_order].set(jnp.arange(slot_count, dtype=jnp.int32))
    matrix = flexibility[0, 0]
    face_width = slot_order.shape[0] // 4
    cases = dual_load.shape[-1]
    sub_count = lax.axis_size("sub")
    sub_id = lax.axis_index("sub")
    sector_count = lax.axis_size("sector")
    sector_id = lax.axis_index("sector")
    inverse_rows = lax.dynamic_slice_in_dim(coarse_inverse, sector_id * corner_count, corner_count, 0)
    inverse_by_shift = jnp.take(
        inverse_rows.reshape(corner_count, sector_count, corner_count),
        (sector_id - jnp.arange(sector_count)) % sector_count,
        axis=1,
    ).reshape(corner_count, sector_count * corner_count)
    multiplier = jnp.zeros_like(dual_load)
    residual = dual_load
    direction = dual_load
    for iteration in range(ITERS):
        rounded = direction[0, 0].astype(jnp.bfloat16)
        lower_sub = passed_along(rounded[0], "sub", 1)
        previous = from_behind(rounded[1], "sector", 1)
        face_stack = jnp.concatenate([-lower_sub, rounded[0], -previous, rounded[1]], axis=0)
        partial_value = jnp.take(face_stack, corners, axis=0)
        pieces = jnp.stack(gathered(partial_value, "sub")).astype(jnp.float32)
        pieces = jnp.take(pieces, (sub_id - jnp.arange(sub_count)) % sub_count, axis=0)
        sector_total = pieces[0]
        for k in range(1, sub_count):
            sector_total = sector_total + pieces[k]
        everything = jnp.concatenate(gathered(sector_total, "sector"), axis=0)
        coarse = jnp.dot(
            inverse_by_shift,
            everything,
            precision=lax.Precision.HIGHEST,
            preferred_element_type=jnp.float32,
        )
        coarse = coarse / sub_count
        correction = jnp.zeros((4 * face_width, cases), jnp.float32).at[corners].add(coarse)
        own_faces = jnp.take(face_stack, own_place, axis=0)
        own_product = jnp.dot(matrix, own_faces, preferred_element_type=jnp.float32)
        product = jnp.take(own_product, slot_order, axis=0) + correction
        outgoing_sub = product[:face_width]
        outgoing_cycle = product[2 * face_width : 3 * face_width]
        upper_next = passed_along(outgoing_sub.astype(jnp.bfloat16), "sub", -1)
        cycle_next = from_behind(outgoing_cycle.astype(jnp.bfloat16), "sector", -1)
        own_sub = product[face_width : 2 * face_width]
        own_cycle = product[3 * face_width :]
        jump_pair = jnp.stack(
            [own_sub - upper_next.astype(jnp.float32), own_cycle - cycle_next.astype(jnp.float32)],
            axis=0,
        )
        image = jump_pair[None, None]
        if iteration == 0:
            both = total(jnp.stack([inner_sum(residual, residual), inner_sum(direction, image)]))
            norm_now, curvature = both[0], both[1]
        else:
            curvature = total(inner_sum(direction, image))
        alpha = norm_now / curvature
        multiplier = multiplier + alpha * direction
        residual = residual - alpha * image
        if iteration + 1 < ITERS:
            norm_next = squares(residual)
            direction = residual + norm_next / norm_now * direction
            norm_now = norm_next
    return (multiplier, residual)


def solution(mesh):
    return jax.shard_map(
        shards,
        mesh=mesh,
        in_specs=(
            P("sector", "sub", None, None, None),
            P("sector", "sub", None, None),
            P("sector", "sub", None),
            P("sector", "sub", None),
            P(),
        ),
        out_specs=(P("sector", "sub", None, None, None), P("sector", "sub", None, None, None)),
        check_vma=False,
    )
```

```python
import jax
import jax.numpy as jnp
from jax import lax
from jax.sharding import PartitionSpec as P

ITERS = 2


def passed_along(x, axis, by):
    count = lax.axis_size(axis)
    pairs = [(i, i + by) for i in range(count) if 0 <= i + by < count]
    return lax.ppermute(x, axis, pairs)


def from_behind(value, axis, steps):
    count = lax.axis_size(axis)
    pairs = [(source, (source + steps) % count) for source in range(count)]
    return lax.ppermute(value, axis, pairs)


def total(x):
    for axis in ("sub", "sector"):
        count = lax.axis_size(axis)
        if count & (count - 1):
            x = lax.psum(x, axis)
            continue
        step = 1
        while step < count:
            x = x + lax.ppermute(x, axis, [(i, i ^ step) for i in range(count)])
            step *= 2
    return x


def gathered(x, axis):
    count = lax.axis_size(axis)
    return [x] + [
        lax.ppermute(x, axis, [(i, (i + k) % count) for i in range(count)]) for k in range(1, count)
    ]


def squares(residual):
    return total(jnp.sum(residual * residual, axis=(0, 1, 2, 3)))


def inner_sum(left, right):
    return jnp.sum(left * right, axis=(0, 1, 2, 3))


def shards(dual_load, flexibility, face_order, corner_index, coarse_inverse):
    slot_order = face_order[0, 0]
    corners = corner_index[0, 0]
    corner_count = corners.shape[0]
    slot_count = slot_order.shape[0]
    own_place = jnp.zeros((slot_count,), jnp.int32).at[slot_order].set(jnp.arange(slot_count, dtype=jnp.int32))
    matrix = flexibility[0, 0]
    face_width = slot_order.shape[0] // 4
    cases = dual_load.shape[-1]
    sub_count = lax.axis_size("sub")
    sub_id = lax.axis_index("sub")
    sector_count = lax.axis_size("sector")
    sector_id = lax.axis_index("sector")
    inverse_rows = lax.dynamic_slice_in_dim(coarse_inverse, sector_id * corner_count, corner_count, 0)
    inverse_by_shift = jnp.take(
        inverse_rows.reshape(corner_count, sector_count, corner_count),
        (sector_id - jnp.arange(sector_count)) % sector_count,
        axis=1,
    ).reshape(corner_count, sector_count * corner_count)
    multiplier = jnp.zeros_like(dual_load)
    residual = dual_load
    direction = dual_load
    for iteration in range(ITERS):
        rounded = direction[0, 0].astype(jnp.bfloat16)
        lower_sub = passed_along(rounded[0], "sub", 1)
        previous = from_behind(rounded[1], "sector", 1)
        face_stack = jnp.concatenate([-lower_sub, rounded[0], -previous, rounded[1]], axis=0)
        partial_value = jnp.take(face_stack, corners, axis=0)
        pieces = gathered(partial_value, "sub")
        own_faces = jnp.take(face_stack, own_place, axis=0)
        own_faces, pieces = lax.optimization_barrier((own_faces, pieces))
        pieces = jnp.stack(pieces).astype(jnp.float32)
        pieces = jnp.take(pieces, (sub_id - jnp.arange(sub_count)) % sub_count, axis=0)
        sector_total = pieces[0]
        for k in range(1, sub_count):
            sector_total = sector_total + pieces[k]
        everything = jnp.concatenate(gathered(sector_total, "sector"), axis=0)
        coarse = jnp.dot(
            inverse_by_shift,
            everything,
            precision=lax.Precision.HIGHEST,
            preferred_element_type=jnp.float32,
        )
        coarse = coarse / sub_count
        correction = jnp.zeros((4 * face_width, cases), jnp.float32).at[corners].add(coarse)
        own_product = jnp.dot(matrix, own_faces, preferred_element_type=jnp.float32)
        product = jnp.take(own_product, slot_order, axis=0) + correction
        outgoing_sub = product[:face_width]
        outgoing_cycle = product[2 * face_width : 3 * face_width]
        upper_next = passed_along(outgoing_sub.astype(jnp.bfloat16), "sub", -1)
        cycle_next = from_behind(outgoing_cycle.astype(jnp.bfloat16), "sector", -1)
        own_sub = product[face_width : 2 * face_width]
        own_cycle = product[3 * face_width :]
        jump_pair = jnp.stack(
            [own_sub - upper_next.astype(jnp.float32), own_cycle - cycle_next.astype(jnp.float32)],
            axis=0,
        )
        image = jump_pair[None, None]
        if iteration == 0:
            both = total(jnp.stack([inner_sum(residual, residual), inner_sum(direction, image)]))
            norm_now, curvature = both[0], both[1]
        else:
            curvature = total(inner_sum(direction, image))
        alpha = norm_now / curvature
        multiplier = multiplier + alpha * direction
        residual = residual - alpha * image
        if iteration + 1 < ITERS:
            norm_next = squares(residual)
            direction = residual + norm_next / norm_now * direction
            norm_now = norm_next
    return (multiplier, residual)


def solution(mesh):
    return jax.shard_map(
        shards,
        mesh=mesh,
        in_specs=(
            P("sector", "sub", None, None, None),
            P("sector", "sub", None, None),
            P("sector", "sub", None),
            P("sector", "sub", None),
            P(),
        ),
        out_specs=(P("sector", "sub", None, None, None), P("sector", "sub", None, None, None)),
        check_vma=False,
    )
```

```python
import jax
import jax.numpy as jnp
from jax import lax
from jax.sharding import PartitionSpec as P

ITERS = 2


def passed_along(x, axis, by):
    count = lax.axis_size(axis)
    pairs = [(i, i + by) for i in range(count) if 0 <= i + by < count]
    return lax.ppermute(x, axis, pairs)


def from_behind(value, axis, steps):
    count = lax.axis_size(axis)
    pairs = [(source, (source + steps) % count) for source in range(count)]
    return lax.ppermute(value, axis, pairs)


def total(x):
    for axis in ("sub", "sector"):
        count = lax.axis_size(axis)
        if count & (count - 1):
            x = lax.psum(x, axis)
            continue
        step = 1
        while step < count:
            x = x + lax.ppermute(x, axis, [(i, i ^ step) for i in range(count)])
            step *= 2
    return x


def gathered(x, axis):
    count = lax.axis_size(axis)
    return [x] + [
        lax.ppermute(x, axis, [(i, (i + k) % count) for i in range(count)]) for k in range(1, count)
    ]


def squares(residual):
    return total(jnp.sum(residual * residual, axis=(0, 1, 2, 3)))


def inner_sum(left, right):
    return jnp.sum(left * right, axis=(0, 1, 2, 3))


def shards(dual_load, flexibility, face_order, corner_index, coarse_inverse):
    slot_order = face_order[0, 0]
    corners = corner_index[0, 0]
    corner_count = corners.shape[0]
    slot_count = slot_order.shape[0]
    own_place = jnp.zeros((slot_count,), jnp.int32).at[slot_order].set(jnp.arange(slot_count, dtype=jnp.int32))
    matrix = flexibility[0, 0]
    face_width = slot_order.shape[0] // 4
    cases = dual_load.shape[-1]
    send_order = jnp.concatenate([slot_order[:face_width], slot_order[2 * face_width : 3 * face_width]])
    keep_order = jnp.concatenate([slot_order[face_width : 2 * face_width], slot_order[3 * face_width :]])
    sub_count = lax.axis_size("sub")
    sub_id = lax.axis_index("sub")
    sector_count = lax.axis_size("sector")
    sector_id = lax.axis_index("sector")
    inverse_rows = lax.dynamic_slice_in_dim(coarse_inverse, sector_id * corner_count, corner_count, 0)
    inverse_by_shift = jnp.take(
        inverse_rows.reshape(corner_count, sector_count, corner_count),
        (sector_id - jnp.arange(sector_count)) % sector_count,
        axis=1,
    ).reshape(corner_count, sector_count * corner_count)
    multiplier = jnp.zeros_like(dual_load)
    residual = dual_load
    direction = dual_load
    for iteration in range(ITERS):
        rounded = direction[0, 0].astype(jnp.bfloat16)
        lower_sub = passed_along(rounded[0], "sub", 1)
        previous = from_behind(rounded[1], "sector", 1)
        face_stack = jnp.concatenate([-lower_sub, rounded[0], -previous, rounded[1]], axis=0)
        partial_value = jnp.take(face_stack, corners, axis=0)
        pieces = gathered(partial_value, "sub")
        own_faces = jnp.take(face_stack, own_place, axis=0)
        own_faces, pieces = lax.optimization_barrier((own_faces, pieces))
        pieces = jnp.stack(pieces).astype(jnp.float32)
        pieces = jnp.take(pieces, (sub_id - jnp.arange(sub_count)) % sub_count, axis=0)
        sector_total = pieces[0]
        for k in range(1, sub_count):
            sector_total = sector_total + pieces[k]
        everything = jnp.concatenate(gathered(sector_total, "sector"), axis=0)
        coarse = jnp.dot(
            inverse_by_shift,
            everything,
            precision=lax.Precision.HIGHEST,
            preferred_element_type=jnp.float32,
        )
        coarse = coarse / sub_count
        correction = jnp.zeros((4 * face_width, cases), jnp.float32).at[corners].add(coarse)
        own_product = jnp.dot(matrix, own_faces, preferred_element_type=jnp.float32)
        outgoing = jnp.take(own_product, send_order, axis=0) + jnp.concatenate(
            [correction[:face_width], correction[2 * face_width : 3 * face_width]], axis=0
        )
        outgoing = outgoing.astype(jnp.bfloat16)
        outgoing, own_product = lax.optimization_barrier((outgoing, own_product))
        upper_next = passed_along(outgoing[:face_width], "sub", -1)
        cycle_next = from_behind(outgoing[face_width:], "sector", -1)
        kept = jnp.take(own_product, keep_order, axis=0) + jnp.concatenate(
            [correction[face_width : 2 * face_width], correction[3 * face_width :]], axis=0
        )
        own_sub = kept[:face_width]
        own_cycle = kept[face_width:]
        jump_pair = jnp.stack(
            [own_sub - upper_next.astype(jnp.float32), own_cycle - cycle_next.astype(jnp.float32)],
            axis=0,
        )
        image = jump_pair[None, None]
        if iteration == 0:
            both = total(jnp.stack([inner_sum(residual, residual), inner_sum(direction, image)]))
            norm_now, curvature = both[0], both[1]
        else:
            curvature = total(inner_sum(direction, image))
        alpha = norm_now / curvature
        multiplier = multiplier + alpha * direction
        residual = residual - alpha * image
        if iteration + 1 < ITERS:
            norm_next = squares(residual)
            direction = residual + norm_next / norm_now * direction
            norm_now = norm_next
    return (multiplier, residual)


def solution(mesh):
    return jax.shard_map(
        shards,
        mesh=mesh,
        in_specs=(
            P("sector", "sub", None, None, None),
            P("sector", "sub", None, None),
            P("sector", "sub", None),
            P("sector", "sub", None),
            P(),
        ),
        out_specs=(P("sector", "sub", None, None, None), P("sector", "sub", None, None, None)),
        check_vma=False,
    )
```

```python
import jax
import jax.numpy as jnp
from jax import lax
from jax.sharding import PartitionSpec as P

ITERS = 2


def passed_along(x, axis, by):
    count = lax.axis_size(axis)
    pairs = [(i, i + by) for i in range(count) if 0 <= i + by < count]
    return lax.ppermute(x, axis, pairs)


def from_behind(value, axis, steps):
    count = lax.axis_size(axis)
    pairs = [(source, (source + steps) % count) for source in range(count)]
    return lax.ppermute(value, axis, pairs)


def total(x):
    for axis in ("sub", "sector"):
        count = lax.axis_size(axis)
        if count & (count - 1):
            x = lax.psum(x, axis)
            continue
        step = 1
        while step < count:
            x = x + lax.ppermute(x, axis, [(i, i ^ step) for i in range(count)])
            step *= 2
    return x


def gathered(x, axis):
    count = lax.axis_size(axis)
    return [x] + [
        lax.ppermute(x, axis, [(i, (i + k) % count) for i in range(count)]) for k in range(1, count)
    ]


def butterfly_sum(x, axis):
    count = lax.axis_size(axis)
    if count & (count - 1):
        return lax.psum(x, axis)
    step = 1
    while step < count:
        x = x + lax.ppermute(x, axis, [(i, i ^ step) for i in range(count)])
        step *= 2
    return x


def butterfly_gather(x, axis):
    count = lax.axis_size(axis)
    if count & (count - 1):
        return lax.all_gather(x, axis, axis=0, tiled=True)
    me = lax.axis_index(axis)
    step = 1
    while step < count:
        other = lax.ppermute(x, axis, [(i, i ^ step) for i in range(count)])
        x = jnp.where((me & step) == 0, jnp.concatenate([x, other]), jnp.concatenate([other, x]))
        step *= 2
    return x


def squares(residual):
    return total(jnp.sum(residual * residual, axis=(0, 1, 2, 3)))


def inner_sum(left, right):
    return jnp.sum(left * right, axis=(0, 1, 2, 3))


def shards(dual_load, flexibility, face_order, corner_index, coarse_inverse):
    slot_order = face_order[0, 0]
    corners = corner_index[0, 0]
    corner_count = corners.shape[0]
    slot_count = slot_order.shape[0]
    own_place = jnp.zeros((slot_count,), jnp.int32).at[slot_order].set(jnp.arange(slot_count, dtype=jnp.int32))
    matrix = flexibility[0, 0]
    face_width = slot_order.shape[0] // 4
    cases = dual_load.shape[-1]
    sub_count = lax.axis_size("sub")
    sub_id = lax.axis_index("sub")
    sector_count = lax.axis_size("sector")
    sector_id = lax.axis_index("sector")
    inverse_rows = lax.dynamic_slice_in_dim(coarse_inverse, sector_id * corner_count, corner_count, 0)
    multiplier = jnp.zeros_like(dual_load)
    residual = dual_load
    direction = dual_load
    for iteration in range(ITERS):
        rounded = direction[0, 0].astype(jnp.bfloat16)
        lower_sub = passed_along(rounded[0], "sub", 1)
        previous = from_behind(rounded[1], "sector", 1)
        face_stack = jnp.concatenate([-lower_sub, rounded[0], -previous, rounded[1]], axis=0)
        partial_value = jnp.take(face_stack, corners, axis=0)
        sector_total = butterfly_sum(partial_value.astype(jnp.float32), "sub")
        own_faces = jnp.take(face_stack, own_place, axis=0)
        own_faces, sector_total = lax.optimization_barrier((own_faces, sector_total))
        everything = butterfly_gather(sector_total, "sector")
        coarse = jnp.dot(
            inverse_rows,
            everything,
            precision=lax.Precision.HIGHEST,
            preferred_element_type=jnp.float32,
        )
        coarse = coarse / sub_count
        correction = jnp.zeros((4 * face_width, cases), jnp.float32).at[corners].add(coarse)
        own_product = jnp.dot(matrix, own_faces, preferred_element_type=jnp.float32)
        product = jnp.take(own_product, slot_order, axis=0) + correction
        outgoing_sub = product[:face_width]
        outgoing_cycle = product[2 * face_width : 3 * face_width]
        upper_next = passed_along(outgoing_sub.astype(jnp.bfloat16), "sub", -1)
        cycle_next = from_behind(outgoing_cycle.astype(jnp.bfloat16), "sector", -1)
        own_sub = product[face_width : 2 * face_width]
        own_cycle = product[3 * face_width :]
        jump_pair = jnp.stack(
            [own_sub - upper_next.astype(jnp.float32), own_cycle - cycle_next.astype(jnp.float32)],
            axis=0,
        )
        image = jump_pair[None, None]
        if iteration == 0:
            both = total(jnp.stack([inner_sum(residual, residual), inner_sum(direction, image)]))
            norm_now, curvature = both[0], both[1]
        else:
            curvature = total(inner_sum(direction, image))
        alpha = norm_now / curvature
        multiplier = multiplier + alpha * direction
        residual = residual - alpha * image
        if iteration + 1 < ITERS:
            norm_next = squares(residual)
            direction = residual + norm_next / norm_now * direction
            norm_now = norm_next
    return (multiplier, residual)


def solution(mesh):
    return jax.shard_map(
        shards,
        mesh=mesh,
        in_specs=(
            P("sector", "sub", None, None, None),
            P("sector", "sub", None, None),
            P("sector", "sub", None),
            P("sector", "sub", None),
            P(),
        ),
        out_specs=(P("sector", "sub", None, None, None), P("sector", "sub", None, None, None)),
        check_vma=False,
    )
```

```python
import jax
import jax.numpy as jnp
from jax import lax
from jax.sharding import PartitionSpec as P

ITERS = 2


def passed_along(x, axis, by):
    count = lax.axis_size(axis)
    pairs = [(i, i + by) for i in range(count) if 0 <= i + by < count]
    return lax.ppermute(x, axis, pairs)


def from_behind(value, axis, steps):
    count = lax.axis_size(axis)
    pairs = [(source, (source + steps) % count) for source in range(count)]
    return lax.ppermute(value, axis, pairs)


def total(x):
    for axis in ("sub", "sector"):
        count = lax.axis_size(axis)
        if count & (count - 1):
            x = lax.psum(x, axis)
            continue
        step = 1
        while step < count:
            x = x + lax.ppermute(x, axis, [(i, i ^ step) for i in range(count)])
            step *= 2
    return x


def gathered(x, axis):
    count = lax.axis_size(axis)
    return [x] + [
        lax.ppermute(x, axis, [(i, (i + k) % count) for i in range(count)]) for k in range(1, count)
    ]


def butterfly_sum(x, axis):
    count = lax.axis_size(axis)
    if count & (count - 1):
        return lax.psum(x, axis)
    step = 1
    while step < count:
        x = x + lax.ppermute(x, axis, [(i, i ^ step) for i in range(count)])
        step *= 2
    return x


def butterfly_gather(x, axis):
    count = lax.axis_size(axis)
    if count & (count - 1):
        return lax.all_gather(x, axis, axis=0, tiled=True)
    me = lax.axis_index(axis)
    step = 1
    while step < count:
        other = lax.ppermute(x, axis, [(i, i ^ step) for i in range(count)])
        x = jnp.where((me & step) == 0, jnp.concatenate([x, other]), jnp.concatenate([other, x]))
        step *= 2
    return x


def squares(residual):
    return total(jnp.sum(residual * residual, axis=(0, 1, 2, 3)))


def inner_sum(left, right):
    return jnp.sum(left * right, axis=(0, 1, 2, 3))


def shards(dual_load, flexibility, face_order, corner_index, coarse_inverse):
    slot_order = face_order[0, 0]
    corners = corner_index[0, 0]
    corner_count = corners.shape[0]
    slot_count = slot_order.shape[0]
    slots = jnp.arange(slot_count, dtype=jnp.int32)
    own_place = jnp.sum(jnp.where(slot_order[None, :] == slots[:, None], slots[None, :], 0), axis=1)
    matrix = flexibility[0, 0]
    face_width = slot_order.shape[0] // 4
    cases = dual_load.shape[-1]
    sub_count = lax.axis_size("sub")
    sub_id = lax.axis_index("sub")
    sector_count = lax.axis_size("sector")
    sector_id = lax.axis_index("sector")
    inverse_rows = lax.dynamic_slice_in_dim(coarse_inverse, sector_id * corner_count, corner_count, 0)
    multiplier = jnp.zeros_like(dual_load)
    residual = dual_load
    direction = dual_load
    for iteration in range(ITERS):
        rounded = direction[0, 0].astype(jnp.bfloat16)
        lower_sub = passed_along(rounded[0], "sub", 1)
        previous = from_behind(rounded[1], "sector", 1)
        face_stack = jnp.concatenate([-lower_sub, rounded[0], -previous, rounded[1]], axis=0)
        partial_value = jnp.take(face_stack, corners, axis=0)
        sector_total = butterfly_sum(partial_value.astype(jnp.float32), "sub")
        own_faces = jnp.take(face_stack, own_place, axis=0)
        own_faces, sector_total = lax.optimization_barrier((own_faces, sector_total))
        everything = butterfly_gather(sector_total, "sector")
        coarse = jnp.dot(
            inverse_rows,
            everything,
            precision=lax.Precision.HIGHEST,
            preferred_element_type=jnp.float32,
        )
        coarse = coarse / sub_count
        correction = jnp.zeros((4 * face_width, cases), jnp.float32).at[corners].add(coarse)
        own_product = jnp.dot(matrix, own_faces, preferred_element_type=jnp.float32)
        product = jnp.take(own_product, slot_order, axis=0) + correction
        outgoing_sub = product[:face_width]
        outgoing_cycle = product[2 * face_width : 3 * face_width]
        upper_next = passed_along(outgoing_sub.astype(jnp.bfloat16), "sub", -1)
        cycle_next = from_behind(outgoing_cycle.astype(jnp.bfloat16), "sector", -1)
        own_sub = product[face_width : 2 * face_width]
        own_cycle = product[3 * face_width :]
        jump_pair = jnp.stack(
            [own_sub - upper_next.astype(jnp.float32), own_cycle - cycle_next.astype(jnp.float32)],
            axis=0,
        )
        image = jump_pair[None, None]
        if iteration == 0:
            both = total(jnp.stack([inner_sum(residual, residual), inner_sum(direction, image)]))
            norm_now, curvature = both[0], both[1]
        else:
            curvature = total(inner_sum(direction, image))
        alpha = norm_now / curvature
        multiplier = multiplier + alpha * direction
        residual = residual - alpha * image
        if iteration + 1 < ITERS:
            norm_next = squares(residual)
            direction = residual + norm_next / norm_now * direction
            norm_now = norm_next
    return (multiplier, residual)


def solution(mesh):
    return jax.shard_map(
        shards,
        mesh=mesh,
        in_specs=(
            P("sector", "sub", None, None, None),
            P("sector", "sub", None, None),
            P("sector", "sub", None),
            P("sector", "sub", None),
            P(),
        ),
        out_specs=(P("sector", "sub", None, None, None), P("sector", "sub", None, None, None)),
        check_vma=False,
    )
```

```python
import jax
import jax.numpy as jnp
from jax import lax
from jax.sharding import PartitionSpec as P

ITERS = 2


def passed_along(x, axis, by):
    count = lax.axis_size(axis)
    pairs = [(i, i + by) for i in range(count) if 0 <= i + by < count]
    return lax.ppermute(x, axis, pairs)


def from_behind(value, axis, steps):
    count = lax.axis_size(axis)
    pairs = [(source, (source + steps) % count) for source in range(count)]
    return lax.ppermute(value, axis, pairs)


def total(x):
    for axis in ("sub", "sector"):
        count = lax.axis_size(axis)
        if count & (count - 1):
            x = lax.psum(x, axis)
            continue
        step = 1
        while step < count:
            x = x + lax.ppermute(x, axis, [(i, i ^ step) for i in range(count)])
            step *= 2
    return x


def gathered(x, axis):
    count = lax.axis_size(axis)
    return [x] + [
        lax.ppermute(x, axis, [(i, (i + k) % count) for i in range(count)]) for k in range(1, count)
    ]


def butterfly_sum(x, axis):
    count = lax.axis_size(axis)
    if count & (count - 1):
        return lax.psum(x, axis)
    step = 1
    while step < count:
        x = x + lax.ppermute(x, axis, [(i, i ^ step) for i in range(count)])
        step *= 2
    return x


def xor_steps(axis):
    count = lax.axis_size(axis)
    return [1 << b for b in reversed(range(count.bit_length() - 1))]


def exchange_sum(x, axis, steps):
    count = lax.axis_size(axis)
    for step in steps:
        x = x + lax.ppermute(x, axis, [(i, i ^ step) for i in range(count)])
    return x


def butterfly_gather(x, axis):
    count = lax.axis_size(axis)
    if count & (count - 1):
        return lax.all_gather(x, axis, axis=0, tiled=True)
    me = lax.axis_index(axis)
    step = 1
    while step < count:
        other = lax.ppermute(x, axis, [(i, i ^ step) for i in range(count)])
        x = jnp.where((me & step) == 0, jnp.concatenate([x, other]), jnp.concatenate([other, x]))
        step *= 2
    return x


def squares(residual):
    return total(jnp.sum(residual * residual, axis=(0, 1, 2, 3)))


def inner_sum(left, right):
    return jnp.sum(left * right, axis=(0, 1, 2, 3))


def shards(dual_load, flexibility, face_order, corner_index, coarse_inverse):
    slot_order = face_order[0, 0]
    corners = corner_index[0, 0]
    corner_count = corners.shape[0]
    slot_count = slot_order.shape[0]
    slots = jnp.arange(slot_count, dtype=jnp.int32)
    own_place = jnp.sum(jnp.where(slot_order[None, :] == slots[:, None], slots[None, :], 0), axis=1)
    matrix = flexibility[0, 0]
    face_width = slot_order.shape[0] // 4
    cases = dual_load.shape[-1]
    sub_count = lax.axis_size("sub")
    sub_id = lax.axis_index("sub")
    sector_count = lax.axis_size("sector")
    sector_id = lax.axis_index("sector")
    inverse_rows = lax.dynamic_slice_in_dim(coarse_inverse, sector_id * corner_count, corner_count, 0)
    multiplier = jnp.zeros_like(dual_load)
    residual = dual_load
    direction = dual_load
    for iteration in range(ITERS):
        rounded = direction[0, 0].astype(jnp.bfloat16)
        lower_sub = passed_along(rounded[0], "sub", 1)
        previous = from_behind(rounded[1], "sector", 1)
        face_stack = jnp.concatenate([-lower_sub, rounded[0], -previous, rounded[1]], axis=0)
        partial_value = jnp.take(face_stack, corners, axis=0)
        partial_value = partial_value.astype(jnp.float32)
        face_stack, partial_value = lax.optimization_barrier((face_stack, partial_value))
        own_faces = jnp.take(face_stack, own_place, axis=0)
        if sub_count & (sub_count - 1) or sub_count < 2:
            sector_total = lax.psum(partial_value, "sub")
        else:
            steps = xor_steps("sub")
            first = exchange_sum(partial_value, "sub", steps[:1])
            own_faces, first = lax.optimization_barrier((own_faces, first))
            sector_total = exchange_sum(first, "sub", steps[1:])
        own_product = jnp.dot(matrix, own_faces, preferred_element_type=jnp.float32)
        own_product, sector_total = lax.optimization_barrier((own_product, sector_total))
        everything = butterfly_gather(sector_total, "sector")
        coarse = jnp.dot(
            inverse_rows,
            everything,
            precision=lax.Precision.HIGHEST,
            preferred_element_type=jnp.float32,
        )
        coarse = coarse / sub_count
        correction = jnp.zeros((4 * face_width, cases), jnp.float32).at[corners].add(coarse)
        product = jnp.take(own_product, slot_order, axis=0) + correction
        outgoing_sub = product[:face_width]
        outgoing_cycle = product[2 * face_width : 3 * face_width]
        upper_next = passed_along(outgoing_sub.astype(jnp.bfloat16), "sub", -1)
        cycle_next = from_behind(outgoing_cycle.astype(jnp.bfloat16), "sector", -1)
        own_sub = product[face_width : 2 * face_width]
        own_cycle = product[3 * face_width :]
        jump_pair = jnp.stack(
            [own_sub - upper_next.astype(jnp.float32), own_cycle - cycle_next.astype(jnp.float32)],
            axis=0,
        )
        image = jump_pair[None, None]
        if iteration == 0:
            both = total(jnp.stack([inner_sum(residual, residual), inner_sum(direction, image)]))
            norm_now, curvature = both[0], both[1]
        else:
            curvature = total(inner_sum(direction, image))
        alpha = norm_now / curvature
        multiplier = multiplier + alpha * direction
        residual = residual - alpha * image
        if iteration + 1 < ITERS:
            norm_next = squares(residual)
            direction = residual + norm_next / norm_now * direction
            norm_now = norm_next
    return (multiplier, residual)


def solution(mesh):
    return jax.shard_map(
        shards,
        mesh=mesh,
        in_specs=(
            P("sector", "sub", None, None, None),
            P("sector", "sub", None, None),
            P("sector", "sub", None),
            P("sector", "sub", None),
            P(),
        ),
        out_specs=(P("sector", "sub", None, None, None), P("sector", "sub", None, None, None)),
        check_vma=False,
    )
```

```python
import jax
import jax.numpy as jnp
from jax import lax
from jax.sharding import PartitionSpec as P

ITERS = 2


def passed_along(x, axis, by):
    count = lax.axis_size(axis)
    pairs = [(i, i + by) for i in range(count) if 0 <= i + by < count]
    return lax.ppermute(x, axis, pairs)


def from_behind(value, axis, steps):
    count = lax.axis_size(axis)
    pairs = [(source, (source + steps) % count) for source in range(count)]
    return lax.ppermute(value, axis, pairs)


def ordered_sum(x, axis):
    count = lax.axis_size(axis)
    pieces = jnp.stack(gathered(x, axis))
    pieces = jnp.take(pieces, (lax.axis_index(axis) - jnp.arange(count)) % count, axis=0)
    result = pieces[0]
    for k in range(1, count):
        result = result + pieces[k]
    return result


def total(x):
    x = ordered_sum(x, "sub")
    for axis in ("sector",):
        count = lax.axis_size(axis)
        if count & (count - 1):
            x = lax.psum(x, axis)
            continue
        step = 1
        while step < count:
            x = x + lax.ppermute(x, axis, [(i, i ^ step) for i in range(count)])
            step *= 2
    return x


def gathered(x, axis):
    count = lax.axis_size(axis)
    return [x] + [
        lax.ppermute(x, axis, [(i, (i + k) % count) for i in range(count)]) for k in range(1, count)
    ]


def butterfly_sum(x, axis):
    count = lax.axis_size(axis)
    if count & (count - 1):
        return lax.psum(x, axis)
    step = 1
    while step < count:
        x = x + lax.ppermute(x, axis, [(i, i ^ step) for i in range(count)])
        step *= 2
    return x


def xor_steps(axis):
    count = lax.axis_size(axis)
    return [1 << b for b in reversed(range(count.bit_length() - 1))]


def exchange_sum(x, axis, steps):
    count = lax.axis_size(axis)
    for step in steps:
        x = x + lax.ppermute(x, axis, [(i, i ^ step) for i in range(count)])
    return x


def butterfly_gather(x, axis):
    count = lax.axis_size(axis)
    if count & (count - 1):
        return lax.all_gather(x, axis, axis=0, tiled=True)
    me = lax.axis_index(axis)
    step = 1
    while step < count:
        other = lax.ppermute(x, axis, [(i, i ^ step) for i in range(count)])
        x = jnp.where((me & step) == 0, jnp.concatenate([x, other]), jnp.concatenate([other, x]))
        step *= 2
    return x


def squares(residual):
    return total(jnp.sum(residual * residual, axis=(0, 1, 2, 3)))


def inner_sum(left, right):
    return jnp.sum(left * right, axis=(0, 1, 2, 3))


def shards(dual_load, flexibility, face_order, corner_index, coarse_inverse):
    slot_order = face_order[0, 0]
    corners = corner_index[0, 0]
    corner_count = corners.shape[0]
    slot_count = slot_order.shape[0]
    slots = jnp.arange(slot_count, dtype=jnp.int32)
    own_place = jnp.sum(jnp.where(slot_order[None, :] == slots[:, None], slots[None, :], 0), axis=1)
    matrix = flexibility[0, 0]
    face_width = slot_order.shape[0] // 4
    cases = dual_load.shape[-1]
    sub_count = lax.axis_size("sub")
    sub_id = lax.axis_index("sub")
    sector_count = lax.axis_size("sector")
    sector_id = lax.axis_index("sector")
    inverse_rows = lax.dynamic_slice_in_dim(coarse_inverse, sector_id * corner_count, corner_count, 0)
    multiplier = jnp.zeros_like(dual_load)
    residual = dual_load
    direction = dual_load
    for iteration in range(ITERS):
        rounded = direction[0, 0].astype(jnp.bfloat16)
        lower_sub = passed_along(rounded[0], "sub", 1)
        previous = from_behind(rounded[1], "sector", 1)
        face_stack = jnp.concatenate([-lower_sub, rounded[0], -previous, rounded[1]], axis=0)
        partial_value = jnp.take(face_stack, corners, axis=0)
        partial_value = partial_value.astype(jnp.float32)
        face_stack, partial_value = lax.optimization_barrier((face_stack, partial_value))
        own_faces = jnp.take(face_stack, own_place, axis=0)
        if sub_count & (sub_count - 1) or sub_count < 2:
            sector_total = lax.psum(partial_value, "sub")
        else:
            steps = xor_steps("sub")
            first = exchange_sum(partial_value, "sub", steps[:1])
            own_faces, first = lax.optimization_barrier((own_faces, first))
            sector_total = exchange_sum(first, "sub", steps[1:])
        own_product = jnp.dot(matrix, own_faces, preferred_element_type=jnp.float32)
        own_product, sector_total = lax.optimization_barrier((own_product, sector_total))
        everything = butterfly_gather(sector_total, "sector")
        coarse = jnp.dot(
            inverse_rows,
            everything,
            precision=lax.Precision.HIGHEST,
            preferred_element_type=jnp.float32,
        )
        coarse = coarse / sub_count
        correction = jnp.zeros((4 * face_width, cases), jnp.float32).at[corners].add(coarse)
        product = jnp.take(own_product, slot_order, axis=0) + correction
        outgoing_sub = product[:face_width]
        outgoing_cycle = product[2 * face_width : 3 * face_width]
        upper_next = passed_along(outgoing_sub.astype(jnp.bfloat16), "sub", -1)
        cycle_next = from_behind(outgoing_cycle.astype(jnp.bfloat16), "sector", -1)
        own_sub = product[face_width : 2 * face_width]
        own_cycle = product[3 * face_width :]
        jump_pair = jnp.stack(
            [own_sub - upper_next.astype(jnp.float32), own_cycle - cycle_next.astype(jnp.float32)],
            axis=0,
        )
        image = jump_pair[None, None]
        if iteration == 0:
            both = total(jnp.stack([inner_sum(residual, residual), inner_sum(direction, image)]))
            norm_now, curvature = both[0], both[1]
        else:
            curvature = total(inner_sum(direction, image))
        alpha = norm_now / curvature
        multiplier = multiplier + alpha * direction
        residual = residual - alpha * image
        if iteration + 1 < ITERS:
            norm_next = squares(residual)
            direction = residual + norm_next / norm_now * direction
            norm_now = norm_next
    return (multiplier, residual)


def solution(mesh):
    return jax.shard_map(
        shards,
        mesh=mesh,
        in_specs=(
            P("sector", "sub", None, None, None),
            P("sector", "sub", None, None),
            P("sector", "sub", None),
            P("sector", "sub", None),
            P(),
        ),
        out_specs=(P("sector", "sub", None, None, None), P("sector", "sub", None, None, None)),
        check_vma=False,
    )
```

```python
import jax
import jax.numpy as jnp
from jax import lax
from jax.sharding import PartitionSpec as P

ITERS = 2


def passed_along(x, axis, by):
    count = lax.axis_size(axis)
    pairs = [(i, i + by) for i in range(count) if 0 <= i + by < count]
    return lax.ppermute(x, axis, pairs)


def from_behind(value, axis, steps):
    count = lax.axis_size(axis)
    pairs = [(source, (source + steps) % count) for source in range(count)]
    return lax.ppermute(value, axis, pairs)


def total(x):
    for axis in ("sub", "sector"):
        count = lax.axis_size(axis)
        if count & (count - 1):
            x = lax.psum(x, axis)
            continue
        step = 1
        while step < count:
            x = x + lax.ppermute(x, axis, [(i, i ^ step) for i in range(count)])
            step *= 2
    return x


def gathered(x, axis):
    count = lax.axis_size(axis)
    return [x] + [
        lax.ppermute(x, axis, [(i, (i + k) % count) for i in range(count)]) for k in range(1, count)
    ]


def butterfly_sum(x, axis):
    count = lax.axis_size(axis)
    if count & (count - 1):
        return lax.psum(x, axis)
    step = 1
    while step < count:
        x = x + lax.ppermute(x, axis, [(i, i ^ step) for i in range(count)])
        step *= 2
    return x


def xor_steps(axis):
    count = lax.axis_size(axis)
    return [1 << b for b in reversed(range(count.bit_length() - 1))]


def exchange_sum(x, axis, steps):
    count = lax.axis_size(axis)
    for step in steps:
        x = x + lax.ppermute(x, axis, [(i, i ^ step) for i in range(count)])
    return x


def butterfly_gather(x, axis):
    count = lax.axis_size(axis)
    if count & (count - 1):
        return lax.all_gather(x, axis, axis=0, tiled=True)
    me = lax.axis_index(axis)
    step = 1
    while step < count:
        other = lax.ppermute(x, axis, [(i, i ^ step) for i in range(count)])
        x = jnp.where((me & step) == 0, jnp.concatenate([x, other]), jnp.concatenate([other, x]))
        step *= 2
    return x


def squares(residual):
    return total(jnp.sum(residual * residual, axis=(0, 1, 2, 3)))


def inner_sum(left, right):
    return jnp.sum(left * right, axis=(0, 1, 2, 3))


def shards(dual_load, flexibility, face_order, corner_index, coarse_inverse):
    slot_order = face_order[0, 0]
    corners = corner_index[0, 0]
    corner_count = corners.shape[0]
    slot_count = slot_order.shape[0]
    slots = jnp.arange(slot_count, dtype=jnp.int32)
    own_place = jnp.sum(jnp.where(slot_order[None, :] == slots[:, None], slots[None, :], 0), axis=1)
    matrix = flexibility[0, 0]
    face_width = slot_order.shape[0] // 4
    cases = dual_load.shape[-1]
    sub_count = lax.axis_size("sub")
    sub_id = lax.axis_index("sub")
    sector_count = lax.axis_size("sector")
    sector_id = lax.axis_index("sector")
    inverse_rows = lax.dynamic_slice_in_dim(coarse_inverse, sector_id * corner_count, corner_count, 0)
    multiplier = jnp.zeros_like(dual_load)
    residual = dual_load
    direction = dual_load
    for iteration in range(ITERS):
        rounded = direction[0, 0].astype(jnp.bfloat16)
        lower_sub = passed_along(rounded[0], "sub", 1)
        previous = from_behind(rounded[1], "sector", 1)
        face_stack = jnp.concatenate([-lower_sub, rounded[0], -previous, rounded[1]], axis=0)
        partial_value = face_stack.at[corners].get(mode="promise_in_bounds")
        partial_value = partial_value.astype(jnp.float32)
        face_stack, partial_value = lax.optimization_barrier((face_stack, partial_value))
        own_faces = face_stack.at[own_place].get(mode="promise_in_bounds")
        if sub_count & (sub_count - 1) or sub_count < 2:
            sector_total = lax.psum(partial_value, "sub")
        else:
            steps = xor_steps("sub")
            first = exchange_sum(partial_value, "sub", steps[:1])
            own_faces, first = lax.optimization_barrier((own_faces, first))
            sector_total = exchange_sum(first, "sub", steps[1:])
        own_product = jnp.dot(matrix, own_faces, preferred_element_type=jnp.float32)
        own_product, sector_total = lax.optimization_barrier((own_product, sector_total))
        everything = butterfly_gather(sector_total, "sector")
        coarse = jnp.dot(
            inverse_rows,
            everything,
            precision=lax.Precision.HIGHEST,
            preferred_element_type=jnp.float32,
        )
        coarse = coarse / sub_count
        correction = jnp.zeros((4 * face_width, cases), jnp.float32).at[corners].add(coarse, mode="promise_in_bounds")
        product = own_product.at[slot_order].get(mode="promise_in_bounds") + correction
        outgoing_sub = product[:face_width]
        outgoing_cycle = product[2 * face_width : 3 * face_width]
        upper_next = passed_along(outgoing_sub.astype(jnp.bfloat16), "sub", -1)
        cycle_next = from_behind(outgoing_cycle.astype(jnp.bfloat16), "sector", -1)
        own_sub = product[face_width : 2 * face_width]
        own_cycle = product[3 * face_width :]
        jump_pair = jnp.stack(
            [own_sub - upper_next.astype(jnp.float32), own_cycle - cycle_next.astype(jnp.float32)],
            axis=0,
        )
        image = jump_pair[None, None]
        if iteration == 0:
            both = total(jnp.stack([inner_sum(residual, residual), inner_sum(direction, image)]))
            norm_now, curvature = both[0], both[1]
        else:
            curvature = total(inner_sum(direction, image))
        alpha = norm_now / curvature
        multiplier = multiplier + alpha * direction
        residual = residual - alpha * image
        if iteration + 1 < ITERS:
            norm_next = squares(residual)
            direction = residual + norm_next / norm_now * direction
            norm_now = norm_next
    return (multiplier, residual)


def solution(mesh):
    return jax.shard_map(
        shards,
        mesh=mesh,
        in_specs=(
            P("sector", "sub", None, None, None),
            P("sector", "sub", None, None),
            P("sector", "sub", None),
            P("sector", "sub", None),
            P(),
        ),
        out_specs=(P("sector", "sub", None, None, None), P("sector", "sub", None, None, None)),
        check_vma=False,
    )
```

```python
import jax
import jax.numpy as jnp
from jax import lax
from jax.sharding import PartitionSpec as P

ITERS = 2


def passed_along(x, axis, by):
    count = lax.axis_size(axis)
    pairs = [(i, i + by) for i in range(count) if 0 <= i + by < count]
    return lax.ppermute(x, axis, pairs)


def from_behind(value, axis, steps):
    count = lax.axis_size(axis)
    pairs = [(source, (source + steps) % count) for source in range(count)]
    return lax.ppermute(value, axis, pairs)


def total(x, carried=None):
    for axis in ("sub", "sector"):
        if axis == "sector" and carried is not None:
            x, carried = lax.optimization_barrier((x, carried))
        count = lax.axis_size(axis)
        if count & (count - 1):
            x = lax.psum(x, axis)
            continue
        step = 1
        while step < count:
            x = x + lax.ppermute(x, axis, [(i, i ^ step) for i in range(count)])
            step *= 2
    return x if carried is None else (x, carried)


def gathered(x, axis):
    count = lax.axis_size(axis)
    return [x] + [
        lax.ppermute(x, axis, [(i, (i + k) % count) for i in range(count)]) for k in range(1, count)
    ]


def butterfly_sum(x, axis):
    count = lax.axis_size(axis)
    if count & (count - 1):
        return lax.psum(x, axis)
    step = 1
    while step < count:
        x = x + lax.ppermute(x, axis, [(i, i ^ step) for i in range(count)])
        step *= 2
    return x


def xor_steps(axis):
    count = lax.axis_size(axis)
    return [1 << b for b in reversed(range(count.bit_length() - 1))]


def exchange_sum(x, axis, steps):
    count = lax.axis_size(axis)
    for step in steps:
        x = x + lax.ppermute(x, axis, [(i, i ^ step) for i in range(count)])
    return x


def butterfly_gather(x, axis):
    count = lax.axis_size(axis)
    if count & (count - 1):
        return lax.all_gather(x, axis, axis=0, tiled=True)
    me = lax.axis_index(axis)
    step = 1
    while step < count:
        other = lax.ppermute(x, axis, [(i, i ^ step) for i in range(count)])
        x = jnp.where((me & step) == 0, jnp.concatenate([x, other]), jnp.concatenate([other, x]))
        step *= 2
    return x


def squares(residual):
    return total(jnp.sum(residual * residual, axis=(0, 1, 2, 3)))


def inner_sum(left, right):
    return jnp.sum(left * right, axis=(0, 1, 2, 3))


def shards(dual_load, flexibility, face_order, corner_index, coarse_inverse):
    slot_order = face_order[0, 0]
    corners = corner_index[0, 0]
    corner_count = corners.shape[0]
    slot_count = slot_order.shape[0]
    slots = jnp.arange(slot_count, dtype=jnp.int32)
    own_place = jnp.sum(jnp.where(slot_order[None, :] == slots[:, None], slots[None, :], 0), axis=1)
    matrix = flexibility[0, 0]
    face_width = slot_order.shape[0] // 4
    cases = dual_load.shape[-1]
    sub_count = lax.axis_size("sub")
    sub_id = lax.axis_index("sub")
    sector_count = lax.axis_size("sector")
    sector_id = lax.axis_index("sector")
    inverse_rows = lax.dynamic_slice_in_dim(coarse_inverse, sector_id * corner_count, corner_count, 0)
    multiplier = jnp.zeros_like(dual_load)
    residual = dual_load
    direction = dual_load
    for iteration in range(ITERS):
        rounded = direction[0, 0].astype(jnp.bfloat16)
        if iteration == 0:
            lower_direction = passed_along(direction[0, 0, 0], "sub", 1)
            previous_direction = from_behind(direction[0, 0, 1], "sector", 1)
        else:
            lower_direction = lower_residual + scale * lower_direction
            previous_direction = previous_residual + scale * previous_direction
        lower_sub = lower_direction.astype(jnp.bfloat16)
        previous = previous_direction.astype(jnp.bfloat16)
        face_stack = jnp.concatenate([-lower_sub, rounded[0], -previous, rounded[1]], axis=0)
        partial_value = jnp.take(face_stack, corners, axis=0)
        partial_value = partial_value.astype(jnp.float32)
        face_stack, partial_value = lax.optimization_barrier((face_stack, partial_value))
        own_faces = jnp.take(face_stack, own_place, axis=0)
        if sub_count & (sub_count - 1) or sub_count < 2:
            sector_total = lax.psum(partial_value, "sub")
        else:
            steps = xor_steps("sub")
            first = exchange_sum(partial_value, "sub", steps[:1])
            own_faces, first = lax.optimization_barrier((own_faces, first))
            sector_total = exchange_sum(first, "sub", steps[1:])
        own_product = jnp.dot(matrix, own_faces, preferred_element_type=jnp.float32)
        own_product, sector_total = lax.optimization_barrier((own_product, sector_total))
        everything = butterfly_gather(sector_total, "sector")
        coarse = jnp.dot(
            inverse_rows,
            everything,
            precision=lax.Precision.HIGHEST,
            preferred_element_type=jnp.float32,
        )
        coarse = coarse / sub_count
        correction = jnp.zeros((4 * face_width, cases), jnp.float32).at[corners].add(coarse)
        product = jnp.take(own_product, slot_order, axis=0) + correction
        outgoing_sub = product[:face_width]
        outgoing_cycle = product[2 * face_width : 3 * face_width]
        upper_next = passed_along(outgoing_sub.astype(jnp.bfloat16), "sub", -1)
        cycle_next = from_behind(outgoing_cycle.astype(jnp.bfloat16), "sector", -1)
        own_sub = product[face_width : 2 * face_width]
        own_cycle = product[3 * face_width :]
        jump_pair = jnp.stack(
            [own_sub - upper_next.astype(jnp.float32), own_cycle - cycle_next.astype(jnp.float32)],
            axis=0,
        )
        image = jump_pair[None, None]
        if iteration == 0:
            both = total(jnp.stack([inner_sum(residual, residual), inner_sum(direction, image)]))
            norm_now, curvature = both[0], both[1]
        else:
            curvature = total(inner_sum(direction, image))
        alpha = norm_now / curvature
        multiplier = multiplier + alpha * direction
        residual = residual - alpha * image
        if iteration + 1 < ITERS:
            lower_residual = passed_along(residual[0, 0, 0], "sub", 1)
            previous_residual = from_behind(residual[0, 0, 1], "sector", 1)
            norm_next, (lower_residual, previous_residual) = total(
                inner_sum(residual, residual), (lower_residual, previous_residual)
            )
            scale = norm_next / norm_now
            direction = residual + scale * direction
            norm_now = norm_next
    return (multiplier, residual)


def solution(mesh):
    return jax.shard_map(
        shards,
        mesh=mesh,
        in_specs=(
            P("sector", "sub", None, None, None),
            P("sector", "sub", None, None),
            P("sector", "sub", None),
            P("sector", "sub", None),
            P(),
        ),
        out_specs=(P("sector", "sub", None, None, None), P("sector", "sub", None, None, None)),
        check_vma=False,
    )
```

```python
import jax
import jax.numpy as jnp
from jax import lax
from jax.experimental import pallas as pl
from jax.sharding import PartitionSpec as P

ITERS = 2


def passed_along(x, axis, by):
    count = lax.axis_size(axis)
    pairs = [(i, i + by) for i in range(count) if 0 <= i + by < count]
    return lax.ppermute(x, axis, pairs)


def from_behind(value, axis, steps):
    count = lax.axis_size(axis)
    pairs = [(source, (source + steps) % count) for source in range(count)]
    return lax.ppermute(value, axis, pairs)


def _product_kernel(a_ref, b_ref, o_ref):
    o_ref[...] = jnp.dot(a_ref[...], b_ref[...], preferred_element_type=jnp.float32)


def matmul(a, b, rows=256):
    n, k = a.shape
    m = b.shape[1]
    rows = min(rows, n)
    return pl.pallas_call(
        _product_kernel,
        out_shape=jax.ShapeDtypeStruct((n, m), jnp.float32),
        grid=(n // rows,),
        in_specs=[pl.BlockSpec((rows, k), lambda i: (i, 0)), pl.BlockSpec((k, m), lambda i: (0, 0))],
        out_specs=pl.BlockSpec((rows, m), lambda i: (i, 0)),
        cost_estimate=pl.CostEstimate(flops=2 * n * k * m, bytes_accessed=2 * (n * k + k * m) + 4 * n * m, transcendentals=0),
    )(a, b)


def total(x):
    for axis in ("sub", "sector"):
        count = lax.axis_size(axis)
        if count & (count - 1):
            x = lax.psum(x, axis)
            continue
        step = 1
        while step < count:
            x = x + lax.ppermute(x, axis, [(i, i ^ step) for i in range(count)])
            step *= 2
    return x


def gathered(x, axis):
    count = lax.axis_size(axis)
    return [x] + [
        lax.ppermute(x, axis, [(i, (i + k) % count) for i in range(count)]) for k in range(1, count)
    ]


def butterfly_sum(x, axis):
    count = lax.axis_size(axis)
    if count & (count - 1):
        return lax.psum(x, axis)
    step = 1
    while step < count:
        x = x + lax.ppermute(x, axis, [(i, i ^ step) for i in range(count)])
        step *= 2
    return x


def xor_steps(axis):
    count = lax.axis_size(axis)
    return [1 << b for b in reversed(range(count.bit_length() - 1))]


def exchange_sum(x, axis, steps):
    count = lax.axis_size(axis)
    for step in steps:
        x = x + lax.ppermute(x, axis, [(i, i ^ step) for i in range(count)])
    return x


def butterfly_gather(x, axis):
    count = lax.axis_size(axis)
    if count & (count - 1):
        return lax.all_gather(x, axis, axis=0, tiled=True)
    me = lax.axis_index(axis)
    step = 1
    while step < count:
        other = lax.ppermute(x, axis, [(i, i ^ step) for i in range(count)])
        x = jnp.where((me & step) == 0, jnp.concatenate([x, other]), jnp.concatenate([other, x]))
        step *= 2
    return x


def squares(residual):
    return total(jnp.sum(residual * residual, axis=(0, 1, 2, 3)))


def inner_sum(left, right):
    return jnp.sum(left * right, axis=(0, 1, 2, 3))


def shards(dual_load, flexibility, face_order, corner_index, coarse_inverse):
    slot_order = face_order[0, 0]
    corners = corner_index[0, 0]
    corner_count = corners.shape[0]
    slot_count = slot_order.shape[0]
    slots = jnp.arange(slot_count, dtype=jnp.int32)
    own_place = jnp.sum(jnp.where(slot_order[None, :] == slots[:, None], slots[None, :], 0), axis=1)
    matrix = flexibility[0, 0]
    face_width = slot_order.shape[0] // 4
    cases = dual_load.shape[-1]
    sub_count = lax.axis_size("sub")
    sub_id = lax.axis_index("sub")
    sector_count = lax.axis_size("sector")
    sector_id = lax.axis_index("sector")
    inverse_rows = lax.dynamic_slice_in_dim(coarse_inverse, sector_id * corner_count, corner_count, 0)
    multiplier = jnp.zeros_like(dual_load)
    residual = dual_load
    direction = dual_load
    for iteration in range(ITERS):
        rounded = direction[0, 0].astype(jnp.bfloat16)
        lower_sub = passed_along(rounded[0], "sub", 1)
        previous = from_behind(rounded[1], "sector", 1)
        face_stack = jnp.concatenate([-lower_sub, rounded[0], -previous, rounded[1]], axis=0)
        partial_value = jnp.take(face_stack, corners, axis=0)
        partial_value = partial_value.astype(jnp.float32)
        face_stack, partial_value = lax.optimization_barrier((face_stack, partial_value))
        own_faces = jnp.take(face_stack, own_place, axis=0)
        if sub_count & (sub_count - 1) or sub_count < 2:
            sector_total = lax.psum(partial_value, "sub")
        else:
            steps = xor_steps("sub")
            first = exchange_sum(partial_value, "sub", steps[:1])
            own_faces, first = lax.optimization_barrier((own_faces, first))
            sector_total = exchange_sum(first, "sub", steps[1:])
        own_product = matmul(matrix, own_faces)
        own_product, sector_total = lax.optimization_barrier((own_product, sector_total))
        everything = butterfly_gather(sector_total, "sector")
        coarse = jnp.dot(
            inverse_rows,
            everything,
            precision=lax.Precision.HIGHEST,
            preferred_element_type=jnp.float32,
        )
        coarse = coarse / sub_count
        correction = jnp.zeros((4 * face_width, cases), jnp.float32).at[corners].add(coarse)
        product = jnp.take(own_product, slot_order, axis=0) + correction
        outgoing_sub = product[:face_width]
        outgoing_cycle = product[2 * face_width : 3 * face_width]
        upper_next = passed_along(outgoing_sub.astype(jnp.bfloat16), "sub", -1)
        cycle_next = from_behind(outgoing_cycle.astype(jnp.bfloat16), "sector", -1)
        own_sub = product[face_width : 2 * face_width]
        own_cycle = product[3 * face_width :]
        jump_pair = jnp.stack(
            [own_sub - upper_next.astype(jnp.float32), own_cycle - cycle_next.astype(jnp.float32)],
            axis=0,
        )
        image = jump_pair[None, None]
        if iteration == 0:
            both = total(jnp.stack([inner_sum(residual, residual), inner_sum(direction, image)]))
            norm_now, curvature = both[0], both[1]
        else:
            curvature = total(inner_sum(direction, image))
        alpha = norm_now / curvature
        multiplier = multiplier + alpha * direction
        residual = residual - alpha * image
        if iteration + 1 < ITERS:
            norm_next = squares(residual)
            direction = residual + norm_next / norm_now * direction
            norm_now = norm_next
    return (multiplier, residual)


def solution(mesh):
    return jax.shard_map(
        shards,
        mesh=mesh,
        in_specs=(
            P("sector", "sub", None, None, None),
            P("sector", "sub", None, None),
            P("sector", "sub", None),
            P("sector", "sub", None),
            P(),
        ),
        out_specs=(P("sector", "sub", None, None, None), P("sector", "sub", None, None, None)),
        check_vma=False,
    )
```

```python
import jax
import jax.numpy as jnp
from jax import lax
from jax.sharding import PartitionSpec as P

ITERS = 2


def passed_along(x, axis, by):
    count = lax.axis_size(axis)
    pairs = [(i, i + by) for i in range(count) if 0 <= i + by < count]
    return lax.ppermute(x, axis, pairs)


def from_behind(value, axis, steps):
    count = lax.axis_size(axis)
    pairs = [(source, (source + steps) % count) for source in range(count)]
    return lax.ppermute(value, axis, pairs)


def total(x):
    subs, sectors = lax.axis_size("sub"), lax.axis_size("sector")
    if subs & (subs - 1) or sectors & (sectors - 1) or subs < 2 or sectors < 2:
        return lax.psum(x, ("sector", "sub"))
    both = ("sector", "sub")
    count = subs * sectors
    me = lax.axis_index("sector") * subs + lax.axis_index("sub")
    flips = (1, subs, subs + 1)
    got = [x] + [lax.ppermute(x, both, [(i, i ^ f) for i in range(count)]) for f in flips]
    stack = jnp.stack(got)
    own = me & (subs + 1)
    order = jnp.array([0, 1, subs, subs + 1], jnp.int32) ^ own
    position = (order & 1) + 2 * (order // subs)
    ordered = jnp.take(stack, position, axis=0)
    x = ((ordered[0] + ordered[1]) + ordered[2]) + ordered[3]
    for axis, first in (("sub", 2), ("sector", 2)):
        step = first
        while step < lax.axis_size(axis):
            x = x + lax.ppermute(x, axis, [(i, i ^ step) for i in range(lax.axis_size(axis))])
            step *= 2
    return x


def gathered(x, axis):
    count = lax.axis_size(axis)
    return [x] + [
        lax.ppermute(x, axis, [(i, (i + k) % count) for i in range(count)]) for k in range(1, count)
    ]


def butterfly_sum(x, axis):
    count = lax.axis_size(axis)
    if count & (count - 1):
        return lax.psum(x, axis)
    step = 1
    while step < count:
        x = x + lax.ppermute(x, axis, [(i, i ^ step) for i in range(count)])
        step *= 2
    return x


def xor_steps(axis):
    count = lax.axis_size(axis)
    return [1 << b for b in reversed(range(count.bit_length() - 1))]


def exchange_sum(x, axis, steps):
    count = lax.axis_size(axis)
    for step in steps:
        x = x + lax.ppermute(x, axis, [(i, i ^ step) for i in range(count)])
    return x


def butterfly_gather(x, axis):
    count = lax.axis_size(axis)
    if count & (count - 1):
        return lax.all_gather(x, axis, axis=0, tiled=True)
    me = lax.axis_index(axis)
    step = 1
    while step < count:
        other = lax.ppermute(x, axis, [(i, i ^ step) for i in range(count)])
        x = jnp.where((me & step) == 0, jnp.concatenate([x, other]), jnp.concatenate([other, x]))
        step *= 2
    return x


def squares(residual):
    return total(jnp.sum(residual * residual, axis=(0, 1, 2, 3)))


def inner_sum(left, right):
    return jnp.sum(left * right, axis=(0, 1, 2, 3))


def shards(dual_load, flexibility, face_order, corner_index, coarse_inverse):
    slot_order = face_order[0, 0]
    corners = corner_index[0, 0]
    corner_count = corners.shape[0]
    slot_count = slot_order.shape[0]
    slots = jnp.arange(slot_count, dtype=jnp.int32)
    own_place = jnp.sum(jnp.where(slot_order[None, :] == slots[:, None], slots[None, :], 0), axis=1)
    matrix = flexibility[0, 0]
    face_width = slot_order.shape[0] // 4
    cases = dual_load.shape[-1]
    sub_count = lax.axis_size("sub")
    sub_id = lax.axis_index("sub")
    sector_count = lax.axis_size("sector")
    sector_id = lax.axis_index("sector")
    inverse_rows = lax.dynamic_slice_in_dim(coarse_inverse, sector_id * corner_count, corner_count, 0)
    multiplier = jnp.zeros_like(dual_load)
    residual = dual_load
    direction = dual_load
    for iteration in range(ITERS):
        rounded = direction[0, 0].astype(jnp.bfloat16)
        lower_sub = passed_along(rounded[0], "sub", 1)
        previous = from_behind(rounded[1], "sector", 1)
        face_stack = jnp.concatenate([-lower_sub, rounded[0], -previous, rounded[1]], axis=0)
        partial_value = jnp.take(face_stack, corners, axis=0)
        partial_value = partial_value.astype(jnp.float32)
        face_stack, partial_value = lax.optimization_barrier((face_stack, partial_value))
        own_faces = jnp.take(face_stack, own_place, axis=0)
        if sub_count & (sub_count - 1) or sub_count < 2:
            sector_total = lax.psum(partial_value, "sub")
        else:
            steps = xor_steps("sub")
            first = exchange_sum(partial_value, "sub", steps[:1])
            own_faces, first = lax.optimization_barrier((own_faces, first))
            sector_total = exchange_sum(first, "sub", steps[1:])
        own_product = jnp.dot(matrix, own_faces, preferred_element_type=jnp.float32)
        own_product, sector_total = lax.optimization_barrier((own_product, sector_total))
        everything = butterfly_gather(sector_total, "sector")
        coarse = jnp.dot(
            inverse_rows,
            everything,
            precision=lax.Precision.HIGHEST,
            preferred_element_type=jnp.float32,
        )
        coarse = coarse / sub_count
        correction = jnp.zeros((4 * face_width, cases), jnp.float32).at[corners].add(coarse)
        product = jnp.take(own_product, slot_order, axis=0) + correction
        outgoing_sub = product[:face_width]
        outgoing_cycle = product[2 * face_width : 3 * face_width]
        upper_next = passed_along(outgoing_sub.astype(jnp.bfloat16), "sub", -1)
        cycle_next = from_behind(outgoing_cycle.astype(jnp.bfloat16), "sector", -1)
        own_sub = product[face_width : 2 * face_width]
        own_cycle = product[3 * face_width :]
        jump_pair = jnp.stack(
            [own_sub - upper_next.astype(jnp.float32), own_cycle - cycle_next.astype(jnp.float32)],
            axis=0,
        )
        image = jump_pair[None, None]
        if iteration == 0:
            both = total(jnp.stack([inner_sum(residual, residual), inner_sum(direction, image)]))
            norm_now, curvature = both[0], both[1]
        else:
            curvature = total(inner_sum(direction, image))
        alpha = norm_now / curvature
        multiplier = multiplier + alpha * direction
        residual = residual - alpha * image
        if iteration + 1 < ITERS:
            norm_next = squares(residual)
            direction = residual + norm_next / norm_now * direction
            norm_now = norm_next
    return (multiplier, residual)


def solution(mesh):
    return jax.shard_map(
        shards,
        mesh=mesh,
        in_specs=(
            P("sector", "sub", None, None, None),
            P("sector", "sub", None, None),
            P("sector", "sub", None),
            P("sector", "sub", None),
            P(),
        ),
        out_specs=(P("sector", "sub", None, None, None), P("sector", "sub", None, None, None)),
        check_vma=False,
    )
```

```python
import jax
import jax.numpy as jnp
from jax import lax
from jax.sharding import PartitionSpec as P

ITERS = 2


def passed_along(x, axis, by):
    count = lax.axis_size(axis)
    pairs = [(i, i + by) for i in range(count) if 0 <= i + by < count]
    return lax.ppermute(x, axis, pairs)


def from_behind(value, axis, steps):
    count = lax.axis_size(axis)
    pairs = [(source, (source + steps) % count) for source in range(count)]
    return lax.ppermute(value, axis, pairs)


def total(x):
    for axis in ("sub", "sector"):
        count = lax.axis_size(axis)
        if count & (count - 1):
            x = lax.psum(x, axis)
            continue
        step = 1
        while step < count:
            x = x + lax.ppermute(x, axis, [(i, i ^ step) for i in range(count)])
            step *= 2
    return x


def gathered(x, axis):
    count = lax.axis_size(axis)
    return [x] + [
        lax.ppermute(x, axis, [(i, (i + k) % count) for i in range(count)]) for k in range(1, count)
    ]


def butterfly_sum(x, axis):
    count = lax.axis_size(axis)
    if count & (count - 1):
        return lax.psum(x, axis)
    step = 1
    while step < count:
        x = x + lax.ppermute(x, axis, [(i, i ^ step) for i in range(count)])
        step *= 2
    return x


def xor_steps(axis):
    count = lax.axis_size(axis)
    return [1 << b for b in reversed(range(count.bit_length() - 1))]


def exchange_sum(x, axis, steps):
    count = lax.axis_size(axis)
    for step in steps:
        x = x + lax.ppermute(x, axis, [(i, i ^ step) for i in range(count)])
    return x


def butterfly_gather(x, axis):
    count = lax.axis_size(axis)
    if count & (count - 1):
        return lax.all_gather(x, axis, axis=0, tiled=True)
    me = lax.axis_index(axis)
    step = 1
    while step < count:
        other = lax.ppermute(x, axis, [(i, i ^ step) for i in range(count)])
        x = jnp.where((me & step) == 0, jnp.concatenate([x, other]), jnp.concatenate([other, x]))
        step *= 2
    return x


def squares(residual):
    return total(jnp.sum(residual * residual, axis=(0, 1, 2, 3)))


def inner_sum(left, right):
    return jnp.sum(left * right, axis=(0, 1, 2, 3))


def shards(dual_load, flexibility, face_order, corner_index, coarse_inverse):
    slot_order = face_order[0, 0]
    corners = corner_index[0, 0]
    corner_count = corners.shape[0]
    slot_count = slot_order.shape[0]
    slots = jnp.arange(slot_count, dtype=jnp.int32)
    own_place = jnp.sum(jnp.where(slot_order[None, :] == slots[:, None], slots[None, :], 0), axis=1)
    matrix = flexibility[0, 0]
    face_width = slot_order.shape[0] // 4
    cases = dual_load.shape[-1]
    sub_count = lax.axis_size("sub")
    sub_id = lax.axis_index("sub")
    sector_count = lax.axis_size("sector")
    sector_id = lax.axis_index("sector")
    inverse_rows = lax.dynamic_slice_in_dim(coarse_inverse, sector_id * corner_count, corner_count, 0)
    multiplier = jnp.zeros_like(dual_load)
    residual = dual_load
    direction = dual_load
    for iteration in range(ITERS):
        rounded = direction[0, 0].astype(jnp.bfloat16)
        lower_sub = passed_along(rounded[0], "sub", 1)
        previous = from_behind(rounded[1], "sector", 1)
        face_stack = jnp.concatenate([-lower_sub, rounded[0], -previous, rounded[1]], axis=0)
        partial_value = face_stack.at[corners].get(mode="promise_in_bounds")
        face_stack, partial_value = lax.optimization_barrier((face_stack, partial_value))
        own_faces = jnp.take(face_stack, own_place, axis=0)
        if sub_count & (sub_count - 1) or sub_count < 2:
            sector_total = lax.psum(partial_value.astype(jnp.float32), "sub")
        else:
            steps = xor_steps("sub")
            first = partial_value.astype(jnp.float32) + lax.ppermute(
                partial_value, "sub", [(i, i ^ steps[0]) for i in range(sub_count)]
            ).astype(jnp.float32)
            own_faces, first = lax.optimization_barrier((own_faces, first))
            sector_total = exchange_sum(first, "sub", steps[1:])
        own_product = jnp.dot(matrix, own_faces, preferred_element_type=jnp.float32)
        own_product, sector_total = lax.optimization_barrier((own_product, sector_total))
        everything = butterfly_gather(sector_total, "sector")
        coarse = jnp.dot(
            inverse_rows,
            everything,
            precision=lax.Precision.HIGHEST,
            preferred_element_type=jnp.float32,
        )
        coarse = coarse / sub_count
        correction = jnp.zeros((4 * face_width, cases), jnp.float32).at[corners].add(coarse)
        product = jnp.take(own_product, slot_order, axis=0) + correction
        outgoing_sub = product[:face_width]
        outgoing_cycle = product[2 * face_width : 3 * face_width]
        upper_next = passed_along(outgoing_sub.astype(jnp.bfloat16), "sub", -1)
        cycle_next = from_behind(outgoing_cycle.astype(jnp.bfloat16), "sector", -1)
        own_sub = product[face_width : 2 * face_width]
        own_cycle = product[3 * face_width :]
        jump_pair = jnp.stack(
            [own_sub - upper_next.astype(jnp.float32), own_cycle - cycle_next.astype(jnp.float32)],
            axis=0,
        )
        image = jump_pair[None, None]
        if iteration == 0:
            both = total(jnp.stack([inner_sum(residual, residual), inner_sum(direction, image)]))
            norm_now, curvature = both[0], both[1]
        else:
            curvature = total(inner_sum(direction, image))
        alpha = norm_now / curvature
        multiplier = multiplier + alpha * direction
        residual = residual - alpha * image
        if iteration + 1 < ITERS:
            norm_next = squares(residual)
            direction = residual + norm_next / norm_now * direction
            norm_now = norm_next
    return (multiplier, residual)


def solution(mesh):
    return jax.shard_map(
        shards,
        mesh=mesh,
        in_specs=(
            P("sector", "sub", None, None, None),
            P("sector", "sub", None, None),
            P("sector", "sub", None),
            P("sector", "sub", None),
            P(),
        ),
        out_specs=(P("sector", "sub", None, None, None), P("sector", "sub", None, None, None)),
        check_vma=False,
    )
```

```python
import jax
import jax.numpy as jnp
from jax import lax
from jax.sharding import PartitionSpec as P

ITERS = 2


def passed_along(x, axis, by):
    count = lax.axis_size(axis)
    pairs = [(i, i + by) for i in range(count) if 0 <= i + by < count]
    return lax.ppermute(x, axis, pairs)


def from_behind(value, axis, steps):
    count = lax.axis_size(axis)
    pairs = [(source, (source + steps) % count) for source in range(count)]
    return lax.ppermute(value, axis, pairs)


def total(x):
    for axis in ("sub", "sector"):
        count = lax.axis_size(axis)
        if count & (count - 1):
            x = lax.psum(x, axis)
            continue
        step = 1
        while step < count:
            x = x + lax.ppermute(x, axis, [(i, i ^ step) for i in range(count)])
            step *= 2
    return x


def gathered(x, axis):
    count = lax.axis_size(axis)
    return [x] + [
        lax.ppermute(x, axis, [(i, (i + k) % count) for i in range(count)]) for k in range(1, count)
    ]


def butterfly_sum(x, axis):
    count = lax.axis_size(axis)
    if count & (count - 1):
        return lax.psum(x, axis)
    step = 1
    while step < count:
        x = x + lax.ppermute(x, axis, [(i, i ^ step) for i in range(count)])
        step *= 2
    return x


def xor_steps(axis):
    count = lax.axis_size(axis)
    return [1 << b for b in reversed(range(count.bit_length() - 1))]


def exchange_sum(x, axis, steps):
    count = lax.axis_size(axis)
    for step in steps:
        x = x + lax.ppermute(x, axis, [(i, i ^ step) for i in range(count)])
    return x


def butterfly_gather(x, axis):
    count = lax.axis_size(axis)
    if count & (count - 1):
        return lax.all_gather(x, axis, axis=0, tiled=True)
    me = lax.axis_index(axis)
    step = 1
    while step < count:
        other = lax.ppermute(x, axis, [(i, i ^ step) for i in range(count)])
        x = jnp.where((me & step) == 0, jnp.concatenate([x, other]), jnp.concatenate([other, x]))
        step *= 2
    return x


def squares(residual):
    return total(jnp.sum(residual * residual, axis=(0, 1, 2, 3)))


def inner_sum(left, right):
    return jnp.sum(left * right, axis=(0, 1, 2, 3))


def shards(dual_load, flexibility, face_order, corner_index, coarse_inverse):
    slot_order = face_order[0, 0]
    corners = corner_index[0, 0]
    corner_count = corners.shape[0]
    slot_count = slot_order.shape[0]
    slots = jnp.arange(slot_count, dtype=jnp.int32)
    own_place = jnp.sum(jnp.where(slot_order[None, :] == slots[:, None], slots[None, :], 0), axis=1)
    matrix = flexibility[0, 0]
    face_width = slot_order.shape[0] // 4
    cases = dual_load.shape[-1]
    sub_count = lax.axis_size("sub")
    sub_id = lax.axis_index("sub")
    sector_count = lax.axis_size("sector")
    sector_id = lax.axis_index("sector")
    inverse_rows = lax.dynamic_slice_in_dim(coarse_inverse, sector_id * corner_count, corner_count, 0)
    multiplier = jnp.zeros_like(dual_load)
    residual = dual_load
    direction = dual_load
    for iteration in range(ITERS):
        rounded = direction[0, 0].astype(jnp.bfloat16)
        lower_sub = passed_along(rounded[0], "sub", 1)
        previous = from_behind(rounded[1], "sector", 1)
        face_stack = jnp.concatenate([-lower_sub, rounded[0], -previous, rounded[1]], axis=0)
        partial_value = face_stack.at[corners].get(mode="promise_in_bounds")
        face_stack, partial_value = lax.optimization_barrier((face_stack, partial_value))
        own_faces = face_stack.at[own_place].get(mode="promise_in_bounds")
        if sub_count & (sub_count - 1) or sub_count < 2:
            sector_total = lax.psum(partial_value.astype(jnp.float32), "sub")
        else:
            steps = xor_steps("sub")
            first = partial_value.astype(jnp.float32) + lax.ppermute(
                partial_value, "sub", [(i, i ^ steps[0]) for i in range(sub_count)]
            ).astype(jnp.float32)
            own_faces, first = lax.optimization_barrier((own_faces, first))
            sector_total = exchange_sum(first, "sub", steps[1:])
        own_product = jnp.dot(matrix, own_faces, preferred_element_type=jnp.float32)
        own_product, sector_total = lax.optimization_barrier((own_product, sector_total))
        everything = butterfly_gather(sector_total, "sector")
        coarse = jnp.dot(
            inverse_rows,
            everything,
            precision=lax.Precision.HIGHEST,
            preferred_element_type=jnp.float32,
        )
        coarse = coarse / sub_count
        correction = jnp.zeros((4 * face_width, cases), jnp.float32).at[corners].add(coarse)
        product = jnp.take(own_product, slot_order, axis=0) + correction
        outgoing_sub = product[:face_width]
        outgoing_cycle = product[2 * face_width : 3 * face_width]
        upper_next = passed_along(outgoing_sub.astype(jnp.bfloat16), "sub", -1)
        cycle_next = from_behind(outgoing_cycle.astype(jnp.bfloat16), "sector", -1)
        own_sub = product[face_width : 2 * face_width]
        own_cycle = product[3 * face_width :]
        jump_pair = jnp.stack(
            [own_sub - upper_next.astype(jnp.float32), own_cycle - cycle_next.astype(jnp.float32)],
            axis=0,
        )
        image = jump_pair[None, None]
        if iteration == 0:
            both = total(jnp.stack([inner_sum(residual, residual), inner_sum(direction, image)]))
            norm_now, curvature = both[0], both[1]
        else:
            curvature = total(inner_sum(direction, image))
        alpha = norm_now / curvature
        multiplier = multiplier + alpha * direction
        residual = residual - alpha * image
        if iteration + 1 < ITERS:
            norm_next = squares(residual)
            direction = residual + norm_next / norm_now * direction
            norm_now = norm_next
    return (multiplier, residual)


def solution(mesh):
    return jax.shard_map(
        shards,
        mesh=mesh,
        in_specs=(
            P("sector", "sub", None, None, None),
            P("sector", "sub", None, None),
            P("sector", "sub", None),
            P("sector", "sub", None),
            P(),
        ),
        out_specs=(P("sector", "sub", None, None, None), P("sector", "sub", None, None, None)),
        check_vma=False,
    )
```

```python
import jax
import jax.numpy as jnp
from jax import lax
from jax.sharding import PartitionSpec as P

ITERS = 2


def passed_along(x, axis, by):
    count = lax.axis_size(axis)
    pairs = [(i, i + by) for i in range(count) if 0 <= i + by < count]
    return lax.ppermute(x, axis, pairs)


def from_behind(value, axis, steps):
    count = lax.axis_size(axis)
    pairs = [(source, (source + steps) % count) for source in range(count)]
    return lax.ppermute(value, axis, pairs)


def total(x):
    for axis in ("sub", "sector"):
        count = lax.axis_size(axis)
        if count & (count - 1):
            x = lax.psum(x, axis)
            continue
        step = 1
        while step < count:
            x = x + lax.ppermute(x, axis, [(i, i ^ step) for i in range(count)])
            step *= 2
    return x


def gathered(x, axis):
    count = lax.axis_size(axis)
    return [x] + [
        lax.ppermute(x, axis, [(i, (i + k) % count) for i in range(count)]) for k in range(1, count)
    ]


def butterfly_sum(x, axis):
    count = lax.axis_size(axis)
    if count & (count - 1):
        return lax.psum(x, axis)
    step = 1
    while step < count:
        x = x + lax.ppermute(x, axis, [(i, i ^ step) for i in range(count)])
        step *= 2
    return x


def xor_steps(axis):
    count = lax.axis_size(axis)
    return [1 << b for b in reversed(range(count.bit_length() - 1))]


def exchange_sum(x, axis, steps):
    count = lax.axis_size(axis)
    for step in steps:
        x = x + lax.ppermute(x, axis, [(i, i ^ step) for i in range(count)])
    return x


def butterfly_gather(x, axis):
    count = lax.axis_size(axis)
    if count & (count - 1):
        return lax.all_gather(x, axis, axis=0, tiled=True)
    me = lax.axis_index(axis)
    step = 1
    while step < count:
        other = lax.ppermute(x, axis, [(i, i ^ step) for i in range(count)])
        x = jnp.where((me & step) == 0, jnp.concatenate([x, other]), jnp.concatenate([other, x]))
        step *= 2
    return x


def squares(residual):
    return total(jnp.sum(residual * residual, axis=(0, 1, 2, 3)))


def inner_sum(left, right):
    return jnp.sum(left * right, axis=(0, 1, 2, 3))


def shards(dual_load, flexibility, face_order, corner_index, coarse_inverse):
    slot_order = face_order[0, 0]
    corners = corner_index[0, 0]
    width = face_order.shape[-1] // 4
    sent_sub = passed_along(corners, "sub", -1)
    upper_slots = jnp.where(sent_sub < width, sent_sub, 4 * width)
    sent_cycle = from_behind(corners, "sector", -1)
    cycle_slots = jnp.where((sent_cycle >= 2 * width) & (sent_cycle < 3 * width), sent_cycle - 2 * width, 4 * width)
    corner_count = corners.shape[0]
    slot_count = slot_order.shape[0]
    slots = jnp.arange(slot_count, dtype=jnp.int32)
    own_place = jnp.sum(jnp.where(slot_order[None, :] == slots[:, None], slots[None, :], 0), axis=1)
    matrix = flexibility[0, 0]
    face_width = slot_order.shape[0] // 4
    cases = dual_load.shape[-1]
    sub_count = lax.axis_size("sub")
    sub_id = lax.axis_index("sub")
    sector_count = lax.axis_size("sector")
    sector_id = lax.axis_index("sector")
    inverse_rows = lax.dynamic_slice_in_dim(coarse_inverse, sector_id * corner_count, corner_count, 0)
    multiplier = jnp.zeros_like(dual_load)
    residual = dual_load
    direction = dual_load
    for iteration in range(ITERS):
        rounded = direction[0, 0].astype(jnp.bfloat16)
        lower_sub = passed_along(rounded[0], "sub", 1)
        previous = from_behind(rounded[1], "sector", 1)
        face_stack = jnp.concatenate([-lower_sub, rounded[0], -previous, rounded[1]], axis=0)
        partial_value = face_stack.at[corners].get(mode="promise_in_bounds")
        face_stack, partial_value = lax.optimization_barrier((face_stack, partial_value))
        own_faces = face_stack.at[own_place].get(mode="promise_in_bounds")
        if sub_count & (sub_count - 1) or sub_count < 2:
            sector_total = lax.psum(partial_value.astype(jnp.float32), "sub")
        else:
            steps = xor_steps("sub")
            first = partial_value.astype(jnp.float32) + lax.ppermute(
                partial_value, "sub", [(i, i ^ steps[0]) for i in range(sub_count)]
            ).astype(jnp.float32)
            own_faces, first = lax.optimization_barrier((own_faces, first))
            sector_total = exchange_sum(first, "sub", steps[1:])
        own_product = jnp.dot(matrix, own_faces, preferred_element_type=jnp.float32)
        own_product, sector_total = lax.optimization_barrier((own_product, sector_total))
        everything = butterfly_gather(sector_total, "sector")
        coarse = jnp.dot(
            inverse_rows,
            everything,
            precision=lax.Precision.HIGHEST,
            preferred_element_type=jnp.float32,
        )
        coarse = coarse / sub_count
        raw = jnp.take(own_product, slot_order, axis=0)
        upper_raw = passed_along(raw[:face_width].astype(jnp.bfloat16), "sub", -1)
        cycle_raw = from_behind(raw[2 * face_width : 3 * face_width].astype(jnp.bfloat16), "sector", -1)
        corner_rows = (raw.at[corners].get(mode="promise_in_bounds") + coarse).astype(jnp.bfloat16)
        upper_rows = passed_along(corner_rows, "sub", -1)
        cycle_rows = from_behind(corner_rows, "sector", -1)
        upper_next = upper_raw.at[upper_slots].set(upper_rows, mode="drop")
        cycle_next = cycle_raw.at[cycle_slots].set(cycle_rows, mode="drop")
        correction = jnp.zeros((4 * face_width, cases), jnp.float32).at[corners].add(coarse)
        product = raw + correction
        own_sub = product[face_width : 2 * face_width]
        own_cycle = product[3 * face_width :]
        jump_pair = jnp.stack(
            [own_sub - upper_next.astype(jnp.float32), own_cycle - cycle_next.astype(jnp.float32)],
            axis=0,
        )
        image = jump_pair[None, None]
        if iteration == 0:
            both = total(jnp.stack([inner_sum(residual, residual), inner_sum(direction, image)]))
            norm_now, curvature = both[0], both[1]
        else:
            curvature = total(inner_sum(direction, image))
        alpha = norm_now / curvature
        multiplier = multiplier + alpha * direction
        residual = residual - alpha * image
        if iteration + 1 < ITERS:
            norm_next = squares(residual)
            direction = residual + norm_next / norm_now * direction
            norm_now = norm_next
    return (multiplier, residual)


def solution(mesh):
    return jax.shard_map(
        shards,
        mesh=mesh,
        in_specs=(
            P("sector", "sub", None, None, None),
            P("sector", "sub", None, None),
            P("sector", "sub", None),
            P("sector", "sub", None),
            P(),
        ),
        out_specs=(P("sector", "sub", None, None, None), P("sector", "sub", None, None, None)),
        check_vma=False,
    )
```
